256 devices in a mesh: dp: 16 (over z, core), expert: 16 (over x, y).
Axes of the slice: x: 4, y: 4, z: 8, core: 2. Of those that a mesh axis runs over, the one named last changes fastest.
Arguments:
- tokens: bfloat16 [32768, 2048], P(('dp', 'expert')), may hold values from -24 to 24
- cotangent: bfloat16 [32768, 2048], P(('dp', 'expert')), may hold values from -6 to 6
- expert_ids: int32 [32768, 2], P(('dp', 'expert')), may hold values from 0 to 15, all different within a row; in each aligned block of 128 rows (0 to 127, 128 to 255, ...) at most 24 rows name the same one
- placed: int32 [16], replicated, may hold values from 0 to 15, as said below
- router_weight: bfloat16 [2048, 16], replicated, may hold values from -0.125 to 0.125
- gate_weight: bfloat16 [16, 2048, 768], P('expert', 'dp'), may hold values from -0.125 to 0.125
- up_weight: bfloat16 [16, 2048, 768], P('expert', 'dp'), may hold values from -0.125 to 0.125
- down_weight: bfloat16 [16, 2048, 768], P('expert', 'dp'), may hold values from -0.21875 to 0.21875
Outputs:
- mixed: bfloat16 [32768, 2048], P(('dp', 'expert'))
- token_grad: bfloat16 [32768, 2048], P(('dp', 'expert'))
- gate_grad: bfloat16 [16, 2048, 768], P('expert', 'dp')
- up_grad: bfloat16 [16, 2048, 768], P('expert', 'dp')
- down_grad: bfloat16 [16, 2048, 768], P('expert', 'dp')
- router_grad: float32 [2048, 16], replicated
The draws below stay inside these ranges and needn't reach their ends.
Inputs may be any that keep to these rules, and one draw needn't show every extreme that they name: `expert_ids`: within the rows of one device (128 tokens, two experts each) no expert is named by more than 24 rows, and in some device some expert is named by exactly 24; a token names two different experts. placed is its own inverse, and placed[d] equals d or differs from d in exactly one bit.
All inputs are finite; a program needn't handle non-finite values.
Results may differ from the reference program's by a relative error of at most 0.018.
Values may be sent and summed in bfloat16 or wider, within the bound.
No kernel may reach another device: no remote copies, remote signals or barrier semaphores. Data moves between devices by JAX's collectives and lax.ppermute only.
A program may use at most 128 MiB of HBM per device.

```python
import math
import jax
import jax.numpy as jnp
import numpy as np
from jax import lax

D = 2048
HID = 768
TOK_DEV = 128
EXPERTS = 16
CAP = 24
TOKENS = 32768
N_DP = 16
N_EXPERT = 16


def draw_placed(key, part):
    labels = jnp.arange(EXPERTS, dtype=jnp.int32)
    level_count = EXPERTS.bit_length() - 1
    order = jax.random.permutation(jax.random.fold_in(key, 3), jnp.arange(level_count, dtype=jnp.int32))
    placed = labels
    unpaired = jnp.ones((EXPERTS,), jnp.int32)
    for position in range(level_count):
        bit_value = jnp.left_shift(jnp.int32(1), order[position]).astype(jnp.int32)
        coins = jax.random.randint(jax.random.fold_in(key, 7 + position), (EXPERTS,), 0, 2)
        mate = jnp.bitwise_xor(labels, bit_value).astype(jnp.int32)
        lower = jnp.minimum(labels, mate)
        joined = (unpaired == 1) & (unpaired[mate] == 1) & (coins[lower] > 0)
        placed = jnp.where(joined, mate, placed)
        unpaired = jnp.where(joined, 0, unpaired)
    return placed.astype(jnp.int32)


def strengthened(entries, key, source, target, shards_of, factor):
    owner, partner = [(jnp.arange(entries.shape[axis_at]) // (entries.shape[axis_at] // shards_of)).reshape([-1 if axis == axis_at else 1 for axis in range(entries.ndim)]) for axis_at in (source, target)]
    chosen = jax.random.permutation(key, shards_of)[partner]
    strong = (owner == chosen) | (owner == (partner + shards_of // 2) % shards_of)
    return jnp.where(strong, factor * entries, entries)


def block_levels(key, dims, cuts, least, top_value):
    factor_of, own = 1.0, jax.random.fold_in(key, 6)
    for axis_at, shards_of in cuts:
        draws = jnp.exp(jax.random.uniform(jax.random.fold_in(own, axis_at), (shards_of,), jnp.float32, least / len(cuts), top_value / len(cuts)))
        factor_of = factor_of * jnp.repeat(draws, dims[axis_at] // shards_of).reshape([-1 if axis == axis_at else 1 for axis in range(len(dims))])
    return factor_of


def assign_block(own_key, own, number, rows, number_of, top, reach, slope):
    order = jax.random.permutation(own_key, number_of)
    crowded, common = load_shares(number_of, rows * top, reach, slope, True), load_shares(number_of, rows * top, reach, slope, False)
    places = jnp.arange(number_of)

    def named(tallies, rotation):
        used = int((tallies > 0).sum())
        fixed = max(1, used // 4)
        shifted = fixed + (places - fixed + rotation * (used - fixed)) % max(1, number_of - fixed)
        return jnp.zeros((number_of,), jnp.int32).at[order[jnp.where(places < fixed, places, shifted)]].set(jnp.asarray(tallies, jnp.int32))

    tallies = jnp.where(number % 4 == 0, named(crowded, number // 4), named(common, number - number // 4 - 1))
    mixed = jax.random.permutation(jax.random.fold_in(own, 3), number_of)
    giver, receiver = mixed[0:number_of // 2 * 2:2], mixed[1:number_of // 2 * 2:2]
    room = jnp.minimum(tallies[giver] - 1, reach - tallies[receiver]) // 2
    room = jnp.where((giver == order[0]) | (receiver == order[0]) | (tallies[receiver] == 0), 0, jnp.maximum(room, 0))
    shifted = jax.random.randint(jax.random.fold_in(own, 4), (number_of // 2,), 0, 1 << 20) % (room + 1)
    tallies = tallies.at[giver].add(-shifted).at[receiver].add(shifted)
    items = jnp.searchsorted(jnp.cumsum(tallies), jnp.arange(rows * top), side="right").astype(jnp.int32)
    table = items.reshape(top, rows).T
    table = table[jax.random.permutation(jax.random.fold_in(own, 1), rows)]
    rotation = jax.random.randint(jax.random.fold_in(own, 2), (rows, 1), 0, top)
    return jnp.take_along_axis(table, (jnp.arange(top)[None, :] + rotation) % top, axis=1)


def load_shares(number_of, total, most, lean, full):
    weights = [(1 << 20) // math.isqrt(standing ** lean) + 1 for standing in range(1, number_of + 1)]
    largest = most if full else min(most, max(-(-total // number_of), total * weights[0] // sum(weights)))
    least = 1 if total - largest >= number_of - 1 else 0
    given, rest = [largest] + [least] * (number_of - 1), total - largest - least * (number_of - 1)
    while rest > 0:
        candidates = [i for i in range(1, number_of) if given[i] < largest] or [i for i in range(1, number_of) if given[i] < most]
        mass, remaining = sum([weights[i] for i in candidates]), rest
        for i in candidates:
            addition = min(most - given[i], max(1, remaining * weights[i] // mass), rest)
            given[i] = given[i] + addition
            rest = rest - addition
    return np.array(given)


def gaussian(own_key, extent, scale, limit, shards=(), kind=jnp.bfloat16):
    array = jax.random.normal(own_key, extent, jnp.float32) * scale
    if len(shards) > 0:
        array = block_levels(own_key, extent, shards, -0.22, 0.18) * array
    return jnp.clip(array, min=-limit, max=limit).astype(kind)


def bell_draw_with(own_key, dims, deviation, bound, shards, heavy, kind=jnp.bfloat16):
    values = deviation * jax.random.normal(own_key, dims, jnp.float32)
    if shards:
        values = values * block_levels(own_key, dims, shards, -0.22, 0.18)
    return jnp.clip(strengthened(values, jax.random.fold_in(own_key, 3), *heavy), -bound, bound).astype(kind)


def setup_inputs(seed: int = 0) -> dict:
    seeds = jax.random.split(jax.random.key(seed), 9)
    tokens = bell_draw_with(seeds[0], (TOKENS, D), 1.0, 24.0, ((0, 256),), (0, 1, 256, 6.0))
    cotangent = gaussian(seeds[1], (TOKENS, D), 1.0, 6.0, ((0, 256),))
    expert_ids_keys = jax.random.split(jax.random.fold_in(seeds[2], 1), TOKENS // TOK_DEV)
    expert_ids_turns = jax.random.permutation(jax.random.fold_in(seeds[2], 3), TOKENS // TOK_DEV)
    expert_ids = jax.vmap(lambda own, number: assign_block(jax.random.fold_in(seeds[2], 2), own, number, TOK_DEV, EXPERTS, 2, CAP, 2))(expert_ids_keys, expert_ids_turns).reshape((TOKENS, 2))
    placed = draw_placed(jax.random.fold_in(seeds[8], 71), 0)
    router_weight = gaussian(seeds[4], (D, EXPERTS), D ** -0.5, 0.125)
    gate_weight = gaussian(seeds[5], (EXPERTS, D, HID), D ** -0.5, 0.125, ((0, 16), (1, 16)))
    up_weight = gaussian(seeds[6], (EXPERTS, D, HID), D ** -0.5, 0.125, ((0, 16), (1, 16)))
    down_weight = gaussian(seeds[7], (EXPERTS, D, HID), HID ** -0.5, 0.21875, ((0, 16), (1, 16)))
    return dict(tokens=tokens, cotangent=cotangent, expert_ids=expert_ids, placed=placed, router_weight=router_weight, gate_weight=gate_weight, up_weight=up_weight, down_weight=down_weight)


def gate_values(logits, picked):
    scores = jax.nn.sigmoid(logits)
    chosen = lax.optimization_barrier(jnp.sum(scores[:, None, :] * picked, axis=2))
    return chosen / lax.optimization_barrier(jnp.sum(chosen, axis=1, keepdims=True))

def slot_numbers(expert_ids, holder, capacity, devices):
    labels = jnp.arange(devices, dtype=jnp.int32)
    member_e = (expert_ids[:, :, None] == labels[None, None, :]).astype(jnp.int32)
    target = lax.optimization_barrier(jnp.sum(member_e * holder[None, None, :], axis=2))
    flat_target = target.reshape(-1)
    member = (flat_target[:, None] == labels[None, :]).astype(jnp.int32)
    ranking = lax.optimization_barrier(jnp.sum((jnp.cumsum(member, axis=0) - 1) * member, axis=1))
    return (flat_target * capacity + ranking).reshape(expert_ids.shape).astype(jnp.int32)

def scatter_rows(per_pair, slot_index, total):
    flat_rows = per_pair.reshape(-1, per_pair.shape[2])
    empty = jnp.zeros((total, per_pair.shape[2]), per_pair.dtype)
    return empty.at[slot_index.reshape(-1)].set(flat_rows)

def to_experts(buffer):
    return buffer.reshape(N_EXPERT, N_EXPERT, CAP, buffer.shape[2]).transpose(1, 0, 2, 3).reshape(N_EXPERT, N_EXPERT * CAP, buffer.shape[2])

def expert_forward(slot_rows, gate_full, up_full, down_full):
    pre_gate = jnp.dot(slot_rows, gate_full, preferred_element_type=jnp.float32)
    pre_up = jnp.dot(slot_rows, up_full, preferred_element_type=jnp.float32)
    hidden = (jax.nn.silu(pre_gate) * pre_up).astype(jnp.bfloat16)
    result = jnp.dot(hidden, down_full.T, preferred_element_type=jnp.float32).astype(jnp.bfloat16)
    return (result, pre_gate, pre_up, hidden)

def expert_backward(slot_rows, d_out, pre_gate, pre_up, gate_full, up_full, down_full):
    d_hidden = jnp.dot(d_out, down_full, preferred_element_type=jnp.float32)
    sigma = jax.nn.sigmoid(pre_gate)
    d_pre_gate = (d_hidden * pre_up * sigma * (1.0 + pre_gate * (1.0 - sigma))).astype(jnp.bfloat16)
    d_pre_up = (d_hidden * pre_gate * sigma).astype(jnp.bfloat16)
    d_rows = jnp.dot(d_pre_gate, gate_full.T, preferred_element_type=jnp.float32)
    d_rows = (d_rows + jnp.dot(d_pre_up, up_full.T, preferred_element_type=jnp.float32)).astype(jnp.bfloat16)
    return (d_rows, d_pre_gate, d_pre_up)

def weight_terms(slot_rows, d_out, hidden, d_pre_gate, d_pre_up, scale):
    gate_term = jnp.dot(slot_rows.T, d_pre_gate, preferred_element_type=jnp.float32) * scale
    up_term = jnp.dot(slot_rows.T, d_pre_up, preferred_element_type=jnp.float32) * scale
    down_term = jnp.dot(d_out.T, hidden, preferred_element_type=jnp.float32) * scale
    return (gate_term, up_term, down_term)

def reference(tokens, cotangent, expert_ids, placed, router_weight, gate_weight, up_weight, down_weight):
    labels = jnp.arange(EXPERTS, dtype=jnp.int32)
    logits = jnp.dot(tokens, router_weight, preferred_element_type=jnp.float32)
    picked = (expert_ids[:, :, None] == labels[None, None, :]).astype(jnp.float32)

    def gate_of(values):
        return gate_values(values, picked)
    gate_vals, gate_vjp = jax.vjp(gate_of, logits)
    grad_scale = (2.0 * TOK_DEV * N_DP) ** (-0.5)
    total = N_EXPERT * CAP
    lead = (N_DP, N_EXPERT, TOK_DEV)
    grouped = (tokens.reshape(lead + (D,)), cotangent.reshape(lead + (D,)), expert_ids.reshape(lead + (2,)), gate_vals.reshape(lead + (2,)))

    def slots_of(group_ids_dev):
        return slot_numbers(group_ids_dev, labels, CAP, N_EXPERT)

    def spread_rows(values_dev, slot_dev):
        spread = jnp.broadcast_to(values_dev[:, None, :], (TOK_DEV, 2, D))
        return scatter_rows(spread, slot_dev, total)

    def place_pairs(pairs_dev, slot_dev):
        return scatter_rows(pairs_dev, slot_dev, total)

    def pick_rows(returned_dev, slot_dev):
        return returned_dev[slot_dev]

    def forward_one(bundle):
        return expert_forward(bundle[0], bundle[1], bundle[2], bundle[3])

    def backward_one(bundle):
        return expert_backward(bundle[0], bundle[1], bundle[2], bundle[3], bundle[4], bundle[5], bundle[6])

    def terms_one(bundle):
        return weight_terms(bundle[0], bundle[1], bundle[2], bundle[3], bundle[4], grad_scale)

    def one_group(carry, inputs):
        group_tokens, group_cot, group_ids, group_gates = inputs
        slot_index = jax.vmap(slots_of)(group_ids)
        inbox = to_experts(jax.vmap(spread_rows)(group_tokens, slot_index))
        result, pre_gate, pre_up, hidden = lax.map(forward_one, (inbox, gate_weight, up_weight, down_weight))
        expert_out = jax.vmap(pick_rows)(to_experts(result), slot_index)
        mixed_grp = lax.optimization_barrier(jnp.sum(group_gates[..., None] * expert_out.astype(jnp.float32), axis=2)).astype(jnp.bfloat16)
        d_gates = lax.optimization_barrier(jnp.sum(group_cot[:, :, None, :].astype(jnp.float32) * expert_out.astype(jnp.float32), axis=3))
        d_out = (group_gates[..., None] * group_cot[:, :, None, :].astype(jnp.float32)).astype(jnp.bfloat16)
        d_inbox = to_experts(jax.vmap(place_pairs)(d_out, slot_index))
        d_rows, d_pre_gate, d_pre_up = lax.map(backward_one, (inbox, d_inbox, pre_gate, pre_up, gate_weight, up_weight, down_weight))
        terms = lax.map(terms_one, (inbox, d_inbox, hidden, d_pre_gate, d_pre_up))
        carry = tuple((acc + lax.optimization_barrier(term.astype(jnp.bfloat16)).astype(jnp.float32) for acc, term in zip(carry, terms)))
        d_expert = lax.optimization_barrier(jnp.sum(jax.vmap(pick_rows)(to_experts(d_rows), slot_index).astype(jnp.float32), axis=2))
        return (carry, (mixed_grp, d_gates, d_expert))
    zeros = jnp.zeros((EXPERTS, D, HID), jnp.float32)
    sums, stacked = lax.scan(one_group, (zeros, zeros, zeros), grouped)
    mixed = stacked[0].reshape(TOKENS, D)
    d_gates = stacked[1].reshape(TOKENS, 2)
    d_expert = stacked[2].reshape(TOKENS, D)
    d_logits = gate_vjp(d_gates)[0].astype(jnp.bfloat16)
    router_grad = jnp.dot(tokens.T, d_logits, preferred_element_type=jnp.float32) * TOKENS ** (-0.5)
    token_grad = (d_expert + jnp.dot(d_logits, router_weight.T, preferred_element_type=jnp.float32)).astype(jnp.bfloat16)
    gate_grad = sums[0].astype(jnp.bfloat16)[placed]
    up_grad = sums[1].astype(jnp.bfloat16)[placed]
    down_grad = sums[2].astype(jnp.bfloat16)[placed]
    return (mixed, token_grad, gate_grad, up_grad, down_grad, router_grad)
```

```python
import jax
import jax.numpy as jnp
from jax import lax
from jax.sharding import PartitionSpec as P


def swapped(array, axis, stride):
    return lax.ppermute(array, axis, [(i, i ^ 1 << stride) for i in range(lax.axis_size(axis))])


def gather_by_exchange(piece, axis):
    count = lax.axis_size(axis)
    copies = jnp.broadcast_to(piece[None], (count,) + piece.shape)
    joined = lax.all_to_all(copies, axis, 0, 0, tiled=True)
    return joined.reshape((count * piece.shape[0],) + piece.shape[1:])


def reduce_router(term):
    groups = lax.axis_size("expert")
    replicas = lax.axis_size("dp")
    rows = term.shape[0]
    parts = lax.all_to_all(
        term.reshape(groups, rows // groups, term.shape[1]), "expert", 0, 0, tiled=True
    )
    piece = jnp.sum(parts, axis=0)
    for bit_level in range(replicas.bit_length() - 1):
        piece = piece + swapped(piece, "dp", bit_level)
    return gather_by_exchange(piece, "expert")


def gate_values(logits, picked):
    scores = jax.nn.sigmoid(logits)
    chosen = jnp.sum(scores[:, None, :] * picked, axis=2)
    return chosen / jnp.sum(chosen, axis=1, keepdims=True)


def slot_numbers(expert_ids, holder, capacity, devices):
    labels = jnp.arange(devices, dtype=jnp.int32)
    member_e = (expert_ids[:, :, None] == labels[None, None, :]).astype(jnp.int32)
    target = jnp.sum(member_e * holder[None, None, :], axis=2)
    flat_target = target.reshape(-1)
    member = (flat_target[:, None] == labels[None, :]).astype(jnp.int32)
    ranking = jnp.sum((jnp.cumsum(member, axis=0) - 1) * member, axis=1)
    return (flat_target * capacity + ranking).reshape(expert_ids.shape)


def scatter_rows(per_pair, slot_index, total):
    flat_rows = per_pair.reshape(-1, per_pair.shape[2])
    empty = jnp.zeros((total, per_pair.shape[2]), per_pair.dtype)
    return empty.at[slot_index.reshape(-1)].set(flat_rows)


def expert_forward(slot_rows, gate_full, up_full, down_full):
    pre_gate = jnp.dot(slot_rows, gate_full, preferred_element_type=jnp.float32)
    pre_up = jnp.dot(slot_rows, up_full, preferred_element_type=jnp.float32)
    hidden = (jax.nn.silu(pre_gate) * pre_up).astype(jnp.bfloat16)
    result = lax.dot_general(
        hidden, down_full, (((1,), (1,)), ((), ())), preferred_element_type=jnp.float32
    )
    return (result.astype(jnp.bfloat16), pre_gate, pre_up, hidden)


def expert_backward(d_out, pre_gate, pre_up, gate_full, up_full, down_full):
    d_hidden = jnp.dot(d_out, down_full, preferred_element_type=jnp.float32)
    sigma = jax.nn.sigmoid(pre_gate)
    d_pre_gate = (d_hidden * pre_up * sigma * (1.0 + pre_gate * (1.0 - sigma))).astype(jnp.bfloat16)
    d_pre_up = (d_hidden * pre_gate * sigma).astype(jnp.bfloat16)
    back_dims = (((1,), (1,)), ((), ()))
    d_rows = lax.dot_general(d_pre_gate, gate_full, back_dims, preferred_element_type=jnp.float32)
    d_rows = d_rows + lax.dot_general(
        d_pre_up, up_full, back_dims, preferred_element_type=jnp.float32
    )
    return (d_rows.astype(jnp.bfloat16), d_pre_gate, d_pre_up)


def contract_rows(left, right):
    return lax.dot_general(
        left, right, (((0,), (0,)), ((), ())), preferred_element_type=jnp.float32
    )


def on_device(
    tokens, cotangent, expert_ids, placed, router_weight, gate_weight, up_weight, down_weight
):
    count = tokens.shape[0]
    width = tokens.shape[1]
    hid_width = gate_weight.shape[2]
    groups = lax.axis_size("expert")
    replicas = lax.axis_size("dp")
    capacity = 3 * count // groups
    total = groups * capacity
    levels = groups.bit_length() - 1
    my_index = lax.axis_index("expert")
    labels = jnp.arange(groups, dtype=jnp.int32)
    partner = jnp.sum(jnp.where(labels == my_index, placed, 0))
    grad_scale = (2.0 * count * replicas) ** (-0.5)
    router_scale = (1.0 * count * replicas * groups) ** (-0.5)
    logits = jnp.dot(tokens, router_weight, preferred_element_type=jnp.float32)
    picked = (expert_ids[:, :, None] == labels[None, None, :]).astype(jnp.float32)

    def gate_of(values):
        return gate_values(values, picked)

    gate_vals, gate_vjp = jax.vjp(gate_of, logits)
    held = jnp.concatenate([gate_weight, up_weight, down_weight], axis=0)
    current = held
    for bit_level in range(levels):
        arrived = swapped(held, "expert", bit_level)
        current = jnp.where(partner == jnp.bitwise_xor(my_index, 1 << bit_level), arrived, current)
    gathered = lax.all_gather(current, "dp", axis=1, tiled=True)
    gate_full, up_full, down_full = (gathered[0], gathered[1], gathered[2])
    slot_index = slot_numbers(expert_ids, placed, capacity, groups)
    spread = jnp.broadcast_to(tokens[:, None, :], (count, 2, width))
    outbox = scatter_rows(spread, slot_index, total).reshape(groups, capacity, width)
    received = lax.all_to_all(outbox, "expert", split_axis=0, concat_axis=0, tiled=True)
    item_count = received.shape[1]
    forward_slot_rows = received.reshape(-1, width)
    result, pre_gate, pre_up, hidden = expert_forward(
        forward_slot_rows, gate_full, up_full, down_full
    )
    result, pre_gate, pre_up, hidden, inbox = (
        result.reshape(groups, item_count, width),
        pre_gate.reshape(groups, item_count, hid_width),
        pre_up.reshape(groups, item_count, hid_width),
        hidden.reshape(groups, item_count, hid_width),
        received,
    )
    returned = lax.all_to_all(result, "expert", split_axis=0, concat_axis=0, tiled=True).reshape(
        total, width
    )
    expert_out = returned[slot_index].astype(jnp.float32)
    mixed = jnp.sum(gate_vals[:, :, None] * expert_out, axis=1).astype(jnp.bfloat16)
    cot_wide = cotangent.astype(jnp.float32)
    d_gates = jnp.sum(cot_wide[:, None, :] * expert_out, axis=2)
    d_out = (gate_vals[:, :, None] * cot_wide[:, None, :]).astype(jnp.bfloat16)
    d_outbox = scatter_rows(d_out, slot_index, total).reshape(groups, capacity, width)
    d_inbox = lax.all_to_all(d_outbox, "expert", split_axis=0, concat_axis=0, tiled=True).reshape(
        total, width
    )
    gate_back, up_back, down_back = (gate_full, up_full, down_full)
    slot_rows = inbox.reshape(total, width)
    hidden_rows = hidden.reshape(total, hid_width)
    d_rows, d_pre_gate, d_pre_up = expert_backward(
        d_inbox,
        pre_gate.reshape(total, hid_width),
        pre_up.reshape(total, hid_width),
        gate_back,
        up_back,
        down_back,
    )
    d_returned = lax.all_to_all(
        d_rows.reshape(groups, capacity, width), "expert", split_axis=0, concat_axis=0, tiled=True
    ).reshape(total, width)
    d_expert = jnp.sum(d_returned[slot_index].astype(jnp.float32), axis=1)
    pieces = [
        contract_rows(slot_rows, d_pre_gate),
        contract_rows(slot_rows, d_pre_up),
        contract_rows(d_inbox, hidden_rows),
    ]
    shares = lax.psum_scatter(
        (jnp.concatenate(pieces, axis=1) * grad_scale).astype(jnp.bfloat16),
        "dp",
        scatter_dimension=0,
        tiled=True,
    ).astype(jnp.float32)
    grad_stack = jnp.stack(
        [shares[:, :hid_width], shares[:, hid_width : 2 * hid_width], shares[:, 2 * hid_width :]],
        axis=0,
    ).astype(jnp.bfloat16)
    d_logits = gate_vjp(d_gates)[0].astype(jnp.bfloat16)
    router_term = contract_rows(tokens, d_logits) * router_scale
    router_grad = reduce_router(router_term)
    router_back = lax.dot_general(
        d_logits, router_weight, (((1,), (1,)), ((), ())), preferred_element_type=jnp.float32
    )
    token_grad = (d_expert + router_back).astype(jnp.bfloat16)
    return (mixed, token_grad, grad_stack[0:1], grad_stack[1:2], grad_stack[2:3], router_grad)


def solution(mesh):
    in_specs = (
        P(("dp", "expert"), None),
        P(("dp", "expert"), None),
        P(("dp", "expert"), None),
        P(),
        P(),
        P("expert", "dp", None),
        P("expert", "dp", None),
        P("expert", "dp", None),
    )
    out_specs = (
        P(("dp", "expert"), None),
        P(("dp", "expert"), None),
        P("expert", "dp", None),
        P("expert", "dp", None),
        P("expert", "dp", None),
        P(),
    )
    return jax.shard_map(
        on_device, mesh=mesh, in_specs=in_specs, out_specs=out_specs, check_vma=False
    )
```

```python
import jax
import jax.numpy as jnp
from jax import lax
from jax.sharding import PartitionSpec as P


def swapped(array, axis, stride):
    return lax.ppermute(array, axis, [(i, i ^ 1 << stride) for i in range(lax.axis_size(axis))])


def gather_by_exchange(piece, axis):
    count = lax.axis_size(axis)
    copies = jnp.broadcast_to(piece[None], (count,) + piece.shape)
    joined = lax.all_to_all(copies, axis, 0, 0, tiled=True)
    return joined.reshape((count * piece.shape[0],) + piece.shape[1:])


def reduce_router(term):
    groups = lax.axis_size("expert")
    replicas = lax.axis_size("dp")
    rows = term.shape[0]
    parts = lax.all_to_all(
        term.reshape(groups, rows // groups, term.shape[1]), "expert", 0, 0, tiled=True
    )
    piece = jnp.sum(parts, axis=0)
    for bit_level in range(replicas.bit_length() - 1):
        piece = piece + swapped(piece, "dp", bit_level)
    return gather_by_exchange(piece, "expert")


def gate_values(logits, picked):
    scores = jax.nn.sigmoid(logits)
    chosen = jnp.sum(scores[:, None, :] * picked, axis=2)
    return chosen / jnp.sum(chosen, axis=1, keepdims=True)


def slot_numbers(expert_ids, holder, capacity, devices):
    labels = jnp.arange(devices, dtype=jnp.int32)
    member_e = (expert_ids[:, :, None] == labels[None, None, :]).astype(jnp.int32)
    target = jnp.sum(member_e * holder[None, None, :], axis=2)
    flat_target = target.reshape(-1)
    member = (flat_target[:, None] == labels[None, :]).astype(jnp.int32)
    ranking = jnp.sum((jnp.cumsum(member, axis=0) - 1) * member, axis=1)
    return (flat_target * capacity + ranking).reshape(expert_ids.shape)


def scatter_rows(per_pair, slot_index, total):
    flat_rows = per_pair.reshape(-1, per_pair.shape[2])
    empty = jnp.zeros((total, per_pair.shape[2]), per_pair.dtype)
    return empty.at[slot_index.reshape(-1)].set(flat_rows)


def expert_forward(slot_rows, gate_full, up_full, down_full):
    pre_gate = jnp.dot(slot_rows, gate_full, preferred_element_type=jnp.float32)
    pre_up = jnp.dot(slot_rows, up_full, preferred_element_type=jnp.float32)
    hidden = (jax.nn.silu(pre_gate) * pre_up).astype(jnp.bfloat16)
    result = lax.dot_general(
        hidden, down_full, (((1,), (1,)), ((), ())), preferred_element_type=jnp.float32
    )
    return (result.astype(jnp.bfloat16), pre_gate, pre_up, hidden)


def expert_backward(d_out, pre_gate, pre_up, gate_full, up_full, down_full):
    d_hidden = jnp.dot(d_out, down_full, preferred_element_type=jnp.float32)
    sigma = jax.nn.sigmoid(pre_gate)
    d_pre_gate = (d_hidden * pre_up * sigma * (1.0 + pre_gate * (1.0 - sigma))).astype(jnp.bfloat16)
    d_pre_up = (d_hidden * pre_gate * sigma).astype(jnp.bfloat16)
    back_dims = (((1,), (1,)), ((), ()))
    d_rows = lax.dot_general(d_pre_gate, gate_full, back_dims, preferred_element_type=jnp.float32)
    d_rows = d_rows + lax.dot_general(
        d_pre_up, up_full, back_dims, preferred_element_type=jnp.float32
    )
    return (d_rows.astype(jnp.bfloat16), d_pre_gate, d_pre_up)


def contract_rows(left, right):
    return lax.dot_general(
        left, right, (((0,), (0,)), ((), ())), preferred_element_type=jnp.float32
    )


def on_device(
    tokens, cotangent, expert_ids, placed, router_weight, gate_weight, up_weight, down_weight
):
    count = tokens.shape[0]
    width = tokens.shape[1]
    hid_width = gate_weight.shape[2]
    groups = lax.axis_size("expert")
    replicas = lax.axis_size("dp")
    capacity = 3 * count // groups
    total = groups * capacity
    levels = groups.bit_length() - 1
    my_index = lax.axis_index("expert")
    labels = jnp.arange(groups, dtype=jnp.int32)
    partner = jnp.sum(jnp.where(labels == my_index, placed, 0))
    grad_scale = (2.0 * count * replicas) ** (-0.5)
    router_scale = (1.0 * count * replicas * groups) ** (-0.5)
    logits = jnp.dot(tokens, router_weight, preferred_element_type=jnp.float32)
    picked = (expert_ids[:, :, None] == labels[None, None, :]).astype(jnp.float32)

    def gate_of(values):
        return gate_values(values, picked)

    gate_vals, gate_vjp = jax.vjp(gate_of, logits)
    held = jnp.concatenate([gate_weight, up_weight, down_weight], axis=0)
    gathered = lax.all_gather(held, "dp", axis=1, tiled=True)
    gate_full, up_full, down_full = (gathered[0], gathered[1], gathered[2])
    slot_index = slot_numbers(expert_ids, labels, capacity, groups)
    spread = jnp.broadcast_to(tokens[:, None, :], (count, 2, width))
    outbox = scatter_rows(spread, slot_index, total).reshape(groups, capacity, width)
    received = lax.all_to_all(outbox, "expert", split_axis=0, concat_axis=0, tiled=True)
    item_count = received.shape[1]
    forward_slot_rows = received.reshape(-1, width)
    result, pre_gate, pre_up, hidden = expert_forward(
        forward_slot_rows, gate_full, up_full, down_full
    )
    result, pre_gate, pre_up, hidden, inbox = (
        result.reshape(groups, item_count, width),
        pre_gate.reshape(groups, item_count, hid_width),
        pre_up.reshape(groups, item_count, hid_width),
        hidden.reshape(groups, item_count, hid_width),
        received,
    )
    returned = lax.all_to_all(result, "expert", split_axis=0, concat_axis=0, tiled=True).reshape(
        total, width
    )
    expert_out = returned[slot_index].astype(jnp.float32)
    mixed = jnp.sum(gate_vals[:, :, None] * expert_out, axis=1).astype(jnp.bfloat16)
    cot_wide = cotangent.astype(jnp.float32)
    d_gates = jnp.sum(cot_wide[:, None, :] * expert_out, axis=2)
    d_out = (gate_vals[:, :, None] * cot_wide[:, None, :]).astype(jnp.bfloat16)
    d_outbox = scatter_rows(d_out, slot_index, total).reshape(groups, capacity, width)
    d_inbox = lax.all_to_all(d_outbox, "expert", split_axis=0, concat_axis=0, tiled=True).reshape(
        total, width
    )
    gate_back, up_back, down_back = (gate_full, up_full, down_full)
    slot_rows = inbox.reshape(total, width)
    hidden_rows = hidden.reshape(total, hid_width)
    d_rows, d_pre_gate, d_pre_up = expert_backward(
        d_inbox,
        pre_gate.reshape(total, hid_width),
        pre_up.reshape(total, hid_width),
        gate_back,
        up_back,
        down_back,
    )
    d_returned = lax.all_to_all(
        d_rows.reshape(groups, capacity, width), "expert", split_axis=0, concat_axis=0, tiled=True
    ).reshape(total, width)
    d_expert = jnp.sum(d_returned[slot_index].astype(jnp.float32), axis=1)
    pieces = [
        contract_rows(slot_rows, d_pre_gate),
        contract_rows(slot_rows, d_pre_up),
        contract_rows(d_inbox, hidden_rows),
    ]
    shares = lax.psum_scatter(
        (jnp.concatenate(pieces, axis=1) * grad_scale).astype(jnp.bfloat16),
        "dp",
        scatter_dimension=0,
        tiled=True,
    ).astype(jnp.float32)
    grad_stack = jnp.stack(
        [shares[:, :hid_width], shares[:, hid_width : 2 * hid_width], shares[:, 2 * hid_width :]],
        axis=0,
    ).astype(jnp.bfloat16)
    home_stack = grad_stack
    for bit_level in range(levels):
        arrived = swapped(home_stack, "expert", bit_level)
        grad_stack = jnp.where(partner == jnp.bitwise_xor(my_index, 1 << bit_level), arrived, grad_stack)
    d_logits = gate_vjp(d_gates)[0].astype(jnp.bfloat16)
    router_term = contract_rows(tokens, d_logits) * router_scale
    router_grad = reduce_router(router_term)
    router_back = lax.dot_general(
        d_logits, router_weight, (((1,), (1,)), ((), ())), preferred_element_type=jnp.float32
    )
    token_grad = (d_expert + router_back).astype(jnp.bfloat16)
    return (mixed, token_grad, grad_stack[0:1], grad_stack[1:2], grad_stack[2:3], router_grad)


def solution(mesh):
    in_specs = (
        P(("dp", "expert"), None),
        P(("dp", "expert"), None),
        P(("dp", "expert"), None),
        P(),
        P(),
        P("expert", "dp", None),
        P("expert", "dp", None),
        P("expert", "dp", None),
    )
    out_specs = (
        P(("dp", "expert"), None),
        P(("dp", "expert"), None),
        P("expert", "dp", None),
        P("expert", "dp", None),
        P("expert", "dp", None),
        P(),
    )
    return jax.shard_map(
        on_device, mesh=mesh, in_specs=in_specs, out_specs=out_specs, check_vma=False
    )
```

```python
import jax
import jax.numpy as jnp
from jax import lax
from jax.sharding import PartitionSpec as P


def swapped(array, axis, stride):
    return lax.ppermute(array, axis, [(i, i ^ 1 << stride) for i in range(lax.axis_size(axis))])


def gather_by_exchange(piece, axis):
    count = lax.axis_size(axis)
    copies = jnp.broadcast_to(piece[None], (count,) + piece.shape)
    joined = lax.all_to_all(copies, axis, 0, 0, tiled=True)
    return joined.reshape((count * piece.shape[0],) + piece.shape[1:])


def reduce_router(term, companion, partner, my_index):
    groups = lax.axis_size("expert")
    replicas = lax.axis_size("dp")
    rows = term.shape[0]
    parts = lax.all_to_all(
        term.reshape(groups, rows // groups, term.shape[1]), "expert", 0, 0, tiled=True
    )
    piece = jnp.sum(parts, axis=0)
    piece, companion = lax.optimization_barrier((piece, companion))
    arrivals = [swapped(companion, "expert", bit_level) for bit_level in range(groups.bit_length() - 1)]
    for bit_level in range(replicas.bit_length() - 1):
        piece = piece + swapped(piece, "dp", bit_level)
    piece, arrivals = lax.optimization_barrier((piece, arrivals))
    chosen = companion
    for bit_level, arrived in enumerate(arrivals):
        chosen = jnp.where(partner == jnp.bitwise_xor(my_index, 1 << bit_level), arrived, chosen)
    return gather_by_exchange(piece, "expert"), chosen


def gate_values(logits, picked):
    scores = jax.nn.sigmoid(logits)
    chosen = jnp.sum(scores[:, None, :] * picked, axis=2)
    return chosen / jnp.sum(chosen, axis=1, keepdims=True)


def slot_numbers(expert_ids, holder, capacity, devices):
    labels = jnp.arange(devices, dtype=jnp.int32)
    member_e = (expert_ids[:, :, None] == labels[None, None, :]).astype(jnp.int32)
    target = jnp.sum(member_e * holder[None, None, :], axis=2)
    flat_target = target.reshape(-1)
    member = (flat_target[:, None] == labels[None, :]).astype(jnp.int32)
    ranking = jnp.sum((jnp.cumsum(member, axis=0) - 1) * member, axis=1)
    return (flat_target * capacity + ranking).reshape(expert_ids.shape)


def scatter_rows(per_pair, slot_index, total):
    flat_rows = per_pair.reshape(-1, per_pair.shape[2])
    empty = jnp.zeros((total, per_pair.shape[2]), per_pair.dtype)
    return empty.at[slot_index.reshape(-1)].set(flat_rows)


def expert_forward(slot_rows, gate_full, up_full, down_full):
    pre_gate = jnp.dot(slot_rows, gate_full, preferred_element_type=jnp.float32)
    pre_up = jnp.dot(slot_rows, up_full, preferred_element_type=jnp.float32)
    hidden = (jax.nn.silu(pre_gate) * pre_up).astype(jnp.bfloat16)
    result = lax.dot_general(
        hidden, down_full, (((1,), (1,)), ((), ())), preferred_element_type=jnp.float32
    )
    return (result.astype(jnp.bfloat16), pre_gate, pre_up, hidden)


def expert_backward(d_out, pre_gate, pre_up, gate_full, up_full, down_full):
    d_hidden = jnp.dot(d_out, down_full, preferred_element_type=jnp.float32)
    sigma = jax.nn.sigmoid(pre_gate)
    d_pre_gate = (d_hidden * pre_up * sigma * (1.0 + pre_gate * (1.0 - sigma))).astype(jnp.bfloat16)
    d_pre_up = (d_hidden * pre_gate * sigma).astype(jnp.bfloat16)
    back_dims = (((1,), (1,)), ((), ()))
    d_rows = lax.dot_general(d_pre_gate, gate_full, back_dims, preferred_element_type=jnp.float32)
    d_rows = d_rows + lax.dot_general(
        d_pre_up, up_full, back_dims, preferred_element_type=jnp.float32
    )
    return (d_rows.astype(jnp.bfloat16), d_pre_gate, d_pre_up)


def contract_rows(left, right):
    return lax.dot_general(
        left, right, (((0,), (0,)), ((), ())), preferred_element_type=jnp.float32
    )


def on_device(
    tokens, cotangent, expert_ids, placed, router_weight, gate_weight, up_weight, down_weight
):
    count = tokens.shape[0]
    width = tokens.shape[1]
    hid_width = gate_weight.shape[2]
    groups = lax.axis_size("expert")
    replicas = lax.axis_size("dp")
    capacity = 3 * count // groups
    total = groups * capacity
    levels = groups.bit_length() - 1
    my_index = lax.axis_index("expert")
    labels = jnp.arange(groups, dtype=jnp.int32)
    partner = jnp.sum(jnp.where(labels == my_index, placed, 0))
    grad_scale = (2.0 * count * replicas) ** (-0.5)
    router_scale = (1.0 * count * replicas * groups) ** (-0.5)
    logits = jnp.dot(tokens, router_weight, preferred_element_type=jnp.float32)
    picked = (expert_ids[:, :, None] == labels[None, None, :]).astype(jnp.float32)

    def gate_of(values):
        return gate_values(values, picked)

    gate_vals, gate_vjp = jax.vjp(gate_of, logits)
    held = jnp.concatenate([gate_weight, up_weight, down_weight], axis=0)
    gathered = lax.all_gather(held, "dp", axis=1, tiled=True)
    gate_full, up_full, down_full = (gathered[0], gathered[1], gathered[2])
    slot_index = slot_numbers(expert_ids, labels, capacity, groups)
    spread = jnp.broadcast_to(tokens[:, None, :], (count, 2, width))
    outbox = scatter_rows(spread, slot_index, total).reshape(groups, capacity, width)
    received = lax.all_to_all(outbox, "expert", split_axis=0, concat_axis=0, tiled=True)
    item_count = received.shape[1]
    forward_slot_rows = received.reshape(-1, width)
    result, pre_gate, pre_up, hidden = expert_forward(
        forward_slot_rows, gate_full, up_full, down_full
    )
    result, pre_gate, pre_up, hidden, inbox = (
        result.reshape(groups, item_count, width),
        pre_gate.reshape(groups, item_count, hid_width),
        pre_up.reshape(groups, item_count, hid_width),
        hidden.reshape(groups, item_count, hid_width),
        received,
    )
    returned = lax.all_to_all(result, "expert", split_axis=0, concat_axis=0, tiled=True).reshape(
        total, width
    )
    expert_out = returned[slot_index].astype(jnp.float32)
    mixed = jnp.sum(gate_vals[:, :, None] * expert_out, axis=1).astype(jnp.bfloat16)
    cot_wide = cotangent.astype(jnp.float32)
    d_gates = jnp.sum(cot_wide[:, None, :] * expert_out, axis=2)
    d_out = (gate_vals[:, :, None] * cot_wide[:, None, :]).astype(jnp.bfloat16)
    d_outbox = scatter_rows(d_out, slot_index, total).reshape(groups, capacity, width)
    d_inbox = lax.all_to_all(d_outbox, "expert", split_axis=0, concat_axis=0, tiled=True).reshape(
        total, width
    )
    gate_back, up_back, down_back = (gate_full, up_full, down_full)
    slot_rows = inbox.reshape(total, width)
    hidden_rows = hidden.reshape(total, hid_width)
    d_rows, d_pre_gate, d_pre_up = expert_backward(
        d_inbox,
        pre_gate.reshape(total, hid_width),
        pre_up.reshape(total, hid_width),
        gate_back,
        up_back,
        down_back,
    )
    d_returned = lax.all_to_all(
        d_rows.reshape(groups, capacity, width), "expert", split_axis=0, concat_axis=0, tiled=True
    ).reshape(total, width)
    d_expert = jnp.sum(d_returned[slot_index].astype(jnp.float32), axis=1)
    pieces = [
        contract_rows(slot_rows, d_pre_gate),
        contract_rows(slot_rows, d_pre_up),
        contract_rows(d_inbox, hidden_rows),
    ]
    shares = lax.psum_scatter(
        (jnp.concatenate(pieces, axis=1) * grad_scale).astype(jnp.bfloat16),
        "dp",
        scatter_dimension=0,
        tiled=True,
    ).astype(jnp.float32)
    grad_stack = jnp.stack(
        [shares[:, :hid_width], shares[:, hid_width : 2 * hid_width], shares[:, 2 * hid_width :]],
        axis=0,
    ).astype(jnp.bfloat16)
    d_logits = gate_vjp(d_gates)[0].astype(jnp.bfloat16)
    router_term = contract_rows(tokens, d_logits) * router_scale
    router_grad, grad_stack = reduce_router(router_term, grad_stack, partner, my_index)
    router_back = lax.dot_general(
        d_logits, router_weight, (((1,), (1,)), ((), ())), preferred_element_type=jnp.float32
    )
    token_grad = (d_expert + router_back).astype(jnp.bfloat16)
    return (mixed, token_grad, grad_stack[0:1], grad_stack[1:2], grad_stack[2:3], router_grad)


def solution(mesh):
    in_specs = (
        P(("dp", "expert"), None),
        P(("dp", "expert"), None),
        P(("dp", "expert"), None),
        P(),
        P(),
        P("expert", "dp", None),
        P("expert", "dp", None),
        P("expert", "dp", None),
    )
    out_specs = (
        P(("dp", "expert"), None),
        P(("dp", "expert"), None),
        P("expert", "dp", None),
        P("expert", "dp", None),
        P("expert", "dp", None),
        P(),
    )
    return jax.shard_map(
        on_device, mesh=mesh, in_specs=in_specs, out_specs=out_specs, check_vma=False
    )
```

```python
import jax
import jax.numpy as jnp
from jax import lax
from jax.sharding import PartitionSpec as P


def swapped(array, axis, stride):
    return lax.ppermute(array, axis, [(i, i ^ 1 << stride) for i in range(lax.axis_size(axis))])


def gather_by_exchange(piece, axis):
    count = lax.axis_size(axis)
    copies = jnp.broadcast_to(piece[None], (count,) + piece.shape)
    joined = lax.all_to_all(copies, axis, 0, 0, tiled=True)
    return joined.reshape((count * piece.shape[0],) + piece.shape[1:])


def reduce_router(term, companion, partner, my_index):
    groups = lax.axis_size("expert")
    replicas = lax.axis_size("dp")
    rows = term.shape[0]
    parts = lax.all_to_all(
        term.reshape(groups, rows // groups, term.shape[1]), "expert", 0, 0, tiled=True
    )
    piece = jnp.sum(parts, axis=0)
    piece, companion = lax.optimization_barrier((piece, companion))
    arrivals = [swapped(companion, "expert", bit_level) for bit_level in range(groups.bit_length() - 1)]
    for bit_level in range(replicas.bit_length() - 1):
        piece = piece + swapped(piece, "dp", bit_level)
    piece, arrivals = lax.optimization_barrier((piece, arrivals))
    chosen = companion
    for bit_level, arrived in enumerate(arrivals):
        chosen = jnp.where(partner == jnp.bitwise_xor(my_index, 1 << bit_level), arrived, chosen)
    return gather_by_exchange(piece, "expert"), chosen


def gate_values(logits, picked):
    scores = jax.nn.sigmoid(logits)
    chosen = jnp.sum(scores[:, None, :] * picked, axis=2)
    return chosen / jnp.sum(chosen, axis=1, keepdims=True)


def slot_numbers(expert_ids, holder, capacity, devices):
    labels = jnp.arange(devices, dtype=jnp.int32)
    member_e = (expert_ids[:, :, None] == labels[None, None, :]).astype(jnp.int32)
    target = jnp.sum(member_e * holder[None, None, :], axis=2)
    flat_target = target.reshape(-1)
    member = (flat_target[:, None] == labels[None, :]).astype(jnp.int32)
    ranking = jnp.sum((jnp.cumsum(member, axis=0) - 1) * member, axis=1)
    return (flat_target * capacity + ranking).reshape(expert_ids.shape)


def scatter_rows(per_pair, slot_index, total):
    flat_rows = per_pair.reshape(-1, per_pair.shape[2])
    empty = jnp.zeros((total, per_pair.shape[2]), per_pair.dtype)
    return empty.at[slot_index.reshape(-1)].set(flat_rows)


def expert_forward(slot_rows, gate_full, up_full, down_full):
    pre_gate = jnp.dot(slot_rows, gate_full, preferred_element_type=jnp.float32)
    pre_up = jnp.dot(slot_rows, up_full, preferred_element_type=jnp.float32)
    hidden = (jax.nn.silu(pre_gate) * pre_up).astype(jnp.bfloat16)
    result = lax.dot_general(
        hidden, down_full, (((1,), (1,)), ((), ())), preferred_element_type=jnp.float32
    )
    return (result.astype(jnp.bfloat16), pre_gate, pre_up, hidden)


def expert_backward(d_out, pre_gate, pre_up, gate_full, up_full, down_full):
    d_hidden = jnp.dot(d_out, down_full, preferred_element_type=jnp.float32)
    sigma = jax.nn.sigmoid(pre_gate)
    d_pre_gate = (d_hidden * pre_up * sigma * (1.0 + pre_gate * (1.0 - sigma))).astype(jnp.bfloat16)
    d_pre_up = (d_hidden * pre_gate * sigma).astype(jnp.bfloat16)
    back_dims = (((1,), (1,)), ((), ()))
    d_rows = lax.dot_general(d_pre_gate, gate_full, back_dims, preferred_element_type=jnp.float32)
    d_rows = d_rows + lax.dot_general(
        d_pre_up, up_full, back_dims, preferred_element_type=jnp.float32
    )
    return (d_rows.astype(jnp.bfloat16), d_pre_gate, d_pre_up)


def contract_rows(left, right):
    return lax.dot_general(
        left, right, (((0,), (0,)), ((), ())), preferred_element_type=jnp.float32
    )


def on_device(
    tokens, cotangent, expert_ids, placed, router_weight, gate_weight, up_weight, down_weight
):
    count = tokens.shape[0]
    width = tokens.shape[1]
    hid_width = gate_weight.shape[2]
    groups = lax.axis_size("expert")
    replicas = lax.axis_size("dp")
    capacity = 3 * count // groups
    total = groups * capacity
    levels = groups.bit_length() - 1
    my_index = lax.axis_index("expert")
    labels = jnp.arange(groups, dtype=jnp.int32)
    partner = jnp.sum(jnp.where(labels == my_index, placed, 0))
    grad_scale = (2.0 * count * replicas) ** (-0.5)
    router_scale = (1.0 * count * replicas * groups) ** (-0.5)
    logits = jnp.dot(tokens, router_weight, preferred_element_type=jnp.float32)
    picked = (expert_ids[:, :, None] == labels[None, None, :]).astype(jnp.float32)

    def gate_of(values):
        return gate_values(values, picked)

    gate_vals, gate_vjp = jax.vjp(gate_of, logits)
    held = jnp.concatenate([gate_weight, up_weight], axis=0)
    gathered = lax.all_gather(held, "dp", axis=1, tiled=True)
    gate_full, up_full = (gathered[0], gathered[1])
    slot_index = slot_numbers(expert_ids, labels, capacity, groups)
    spread = jnp.broadcast_to(tokens[:, None, :], (count, 2, width))
    outbox = scatter_rows(spread, slot_index, total).reshape(groups, capacity, width)
    received = lax.all_to_all(outbox, "expert", split_axis=0, concat_axis=0, tiled=True)
    cot_wide = cotangent.astype(jnp.float32)
    d_out = (gate_vals[:, :, None] * cot_wide[:, None, :]).astype(jnp.bfloat16)
    d_outbox = scatter_rows(d_out, slot_index, total).reshape(groups, capacity, width)
    down_held, d_outbox = lax.optimization_barrier((down_weight, d_outbox))
    down_full = lax.all_gather(down_held, "dp", axis=1, tiled=True)[0]
    item_count = received.shape[1]
    forward_slot_rows = received.reshape(-1, width)
    result, pre_gate, pre_up, hidden = expert_forward(
        forward_slot_rows, gate_full, up_full, down_full
    )
    result, pre_gate, pre_up, hidden, inbox = (
        result.reshape(groups, item_count, width),
        pre_gate.reshape(groups, item_count, hid_width),
        pre_up.reshape(groups, item_count, hid_width),
        hidden.reshape(groups, item_count, hid_width),
        received,
    )
    returned = lax.all_to_all(result, "expert", split_axis=0, concat_axis=0, tiled=True).reshape(
        total, width
    )
    expert_out = returned[slot_index].astype(jnp.float32)
    mixed = jnp.sum(gate_vals[:, :, None] * expert_out, axis=1).astype(jnp.bfloat16)
    d_gates = jnp.sum(cot_wide[:, None, :] * expert_out, axis=2)
    d_inbox = lax.all_to_all(d_outbox, "expert", split_axis=0, concat_axis=0, tiled=True).reshape(
        total, width
    )
    gate_back, up_back, down_back = (gate_full, up_full, down_full)
    slot_rows = inbox.reshape(total, width)
    hidden_rows = hidden.reshape(total, hid_width)
    d_rows, d_pre_gate, d_pre_up = expert_backward(
        d_inbox,
        pre_gate.reshape(total, hid_width),
        pre_up.reshape(total, hid_width),
        gate_back,
        up_back,
        down_back,
    )
    d_returned = lax.all_to_all(
        d_rows.reshape(groups, capacity, width), "expert", split_axis=0, concat_axis=0, tiled=True
    ).reshape(total, width)
    d_expert = jnp.sum(d_returned[slot_index].astype(jnp.float32), axis=1)
    pieces = [
        contract_rows(slot_rows, d_pre_gate),
        contract_rows(slot_rows, d_pre_up),
        contract_rows(d_inbox, hidden_rows),
    ]
    shares = lax.psum_scatter(
        (jnp.concatenate(pieces, axis=1) * grad_scale).astype(jnp.bfloat16),
        "dp",
        scatter_dimension=0,
        tiled=True,
    ).astype(jnp.float32)
    grad_stack = jnp.stack(
        [shares[:, :hid_width], shares[:, hid_width : 2 * hid_width], shares[:, 2 * hid_width :]],
        axis=0,
    ).astype(jnp.bfloat16)
    d_logits = gate_vjp(d_gates)[0].astype(jnp.bfloat16)
    router_term = contract_rows(tokens, d_logits) * router_scale
    router_grad, grad_stack = reduce_router(router_term, grad_stack, partner, my_index)
    router_back = lax.dot_general(
        d_logits, router_weight, (((1,), (1,)), ((), ())), preferred_element_type=jnp.float32
    )
    token_grad = (d_expert + router_back).astype(jnp.bfloat16)
    return (mixed, token_grad, grad_stack[0:1], grad_stack[1:2], grad_stack[2:3], router_grad)


def solution(mesh):
    in_specs = (
        P(("dp", "expert"), None),
        P(("dp", "expert"), None),
        P(("dp", "expert"), None),
        P(),
        P(),
        P("expert", "dp", None),
        P("expert", "dp", None),
        P("expert", "dp", None),
    )
    out_specs = (
        P(("dp", "expert"), None),
        P(("dp", "expert"), None),
        P("expert", "dp", None),
        P("expert", "dp", None),
        P("expert", "dp", None),
        P(),
    )
    return jax.shard_map(
        on_device, mesh=mesh, in_specs=in_specs, out_specs=out_specs, check_vma=False
    )
```

```python
import jax
import jax.numpy as jnp
from jax import lax
from jax.sharding import PartitionSpec as P
from jax.experimental.layout import Layout, with_layout_constraint


def swapped(array, axis, stride):
    return lax.ppermute(array, axis, [(i, i ^ 1 << stride) for i in range(lax.axis_size(axis))])


def gather_by_exchange(piece, axis):
    count = lax.axis_size(axis)
    copies = jnp.broadcast_to(piece[None], (count,) + piece.shape)
    joined = lax.all_to_all(copies, axis, 0, 0, tiled=True)
    return joined.reshape((count * piece.shape[0],) + piece.shape[1:])


def reduce_router(term, companion, partner, my_index):
    groups = lax.axis_size("expert")
    replicas = lax.axis_size("dp")
    rows = term.shape[0]
    parts = lax.all_to_all(
        term.reshape(groups, rows // groups, term.shape[1]), "expert", 0, 0, tiled=True
    )
    piece = jnp.sum(parts, axis=0)
    piece, companion = lax.optimization_barrier((piece, companion))
    arrivals = [swapped(companion, "expert", bit_level) for bit_level in range(groups.bit_length() - 1)]
    for bit_level in range(replicas.bit_length() - 1):
        piece = piece + swapped(piece, "dp", bit_level)
    piece, arrivals = lax.optimization_barrier((piece, arrivals))
    chosen = companion
    for bit_level, arrived in enumerate(arrivals):
        chosen = jnp.where(partner == jnp.bitwise_xor(my_index, 1 << bit_level), arrived, chosen)
    return gather_by_exchange(piece, "expert"), chosen


def gate_values(logits, picked):
    scores = jax.nn.sigmoid(logits)
    chosen = jnp.sum(scores[:, None, :] * picked, axis=2)
    return chosen / jnp.sum(chosen, axis=1, keepdims=True)


def slot_numbers(expert_ids, holder, capacity, devices):
    labels = jnp.arange(devices, dtype=jnp.int32)
    member_e = (expert_ids[:, :, None] == labels[None, None, :]).astype(jnp.int32)
    target = jnp.sum(member_e * holder[None, None, :], axis=2)
    flat_target = target.reshape(-1)
    member = (flat_target[:, None] == labels[None, :]).astype(jnp.int32)
    ranking = jnp.sum((jnp.cumsum(member, axis=0) - 1) * member, axis=1)
    return (flat_target * capacity + ranking).reshape(expert_ids.shape)


def scatter_rows(per_pair, slot_index, total):
    flat_rows = per_pair.reshape(-1, per_pair.shape[2])
    empty = jnp.zeros((total, per_pair.shape[2]), per_pair.dtype)
    return empty.at[slot_index.reshape(-1)].set(flat_rows)


def expert_forward(slot_rows, gate_full, up_full, down_full):
    pre_gate = jnp.dot(slot_rows, gate_full, preferred_element_type=jnp.float32)
    pre_up = jnp.dot(slot_rows, up_full, preferred_element_type=jnp.float32)
    hidden = (jax.nn.silu(pre_gate) * pre_up).astype(jnp.bfloat16)
    result = lax.dot_general(
        hidden, down_full, (((1,), (1,)), ((), ())), preferred_element_type=jnp.float32
    )
    return (result.astype(jnp.bfloat16), pre_gate, pre_up, hidden)


def expert_backward(d_out, pre_gate, pre_up, gate_full, up_full, down_full):
    d_hidden = jnp.dot(d_out, down_full, preferred_element_type=jnp.float32)
    sigma = jax.nn.sigmoid(pre_gate)
    d_pre_gate = (d_hidden * pre_up * sigma * (1.0 + pre_gate * (1.0 - sigma))).astype(jnp.bfloat16)
    d_pre_up = (d_hidden * pre_gate * sigma).astype(jnp.bfloat16)
    back_dims = (((1,), (1,)), ((), ()))
    d_rows = lax.dot_general(d_pre_gate, gate_full, back_dims, preferred_element_type=jnp.float32)
    d_rows = d_rows + lax.dot_general(
        d_pre_up, up_full, back_dims, preferred_element_type=jnp.float32
    )
    return (d_rows.astype(jnp.bfloat16), d_pre_gate, d_pre_up)


def row_major(array):
    return with_layout_constraint(array, Layout(major_to_minor=tuple(range(array.ndim))))


def contract_rows(left, right):
    return lax.dot_general(
        left, right, (((0,), (0,)), ((), ())), preferred_element_type=jnp.float32
    )


def on_device(
    tokens, cotangent, expert_ids, placed, router_weight, gate_weight, up_weight, down_weight
):
    count = tokens.shape[0]
    width = tokens.shape[1]
    hid_width = gate_weight.shape[2]
    groups = lax.axis_size("expert")
    replicas = lax.axis_size("dp")
    capacity = 3 * count // groups
    total = groups * capacity
    levels = groups.bit_length() - 1
    my_index = lax.axis_index("expert")
    labels = jnp.arange(groups, dtype=jnp.int32)
    partner = jnp.sum(jnp.where(labels == my_index, placed, 0))
    grad_scale = (2.0 * count * replicas) ** (-0.5)
    router_scale = (1.0 * count * replicas * groups) ** (-0.5)
    logits = jnp.dot(tokens, router_weight, preferred_element_type=jnp.float32)
    picked = (expert_ids[:, :, None] == labels[None, None, :]).astype(jnp.float32)

    def gate_of(values):
        return gate_values(values, picked)

    gate_vals, gate_vjp = jax.vjp(gate_of, logits)
    held = jnp.concatenate([gate_weight, up_weight, down_weight], axis=0)
    gathered = lax.all_gather(held, "dp", axis=1, tiled=True)
    gate_full, up_full, down_full = (gathered[0], gathered[1], gathered[2])
    slot_index = slot_numbers(expert_ids, labels, capacity, groups)
    spread = jnp.broadcast_to(tokens[:, None, :], (count, 2, width))
    outbox = scatter_rows(spread, slot_index, total).reshape(groups, capacity, width)
    received = lax.all_to_all(outbox, "expert", split_axis=0, concat_axis=0, tiled=True)
    item_count = received.shape[1]
    forward_slot_rows = received.reshape(-1, width)
    result, pre_gate, pre_up, hidden = expert_forward(
        forward_slot_rows, gate_full, up_full, down_full
    )
    result, pre_gate, pre_up, hidden, inbox = (
        result.reshape(groups, item_count, width),
        pre_gate.reshape(groups, item_count, hid_width),
        pre_up.reshape(groups, item_count, hid_width),
        hidden.reshape(groups, item_count, hid_width),
        received,
    )
    returned = lax.all_to_all(result, "expert", split_axis=0, concat_axis=0, tiled=True).reshape(
        total, width
    )
    expert_out = returned[slot_index].astype(jnp.float32)
    mixed = jnp.sum(gate_vals[:, :, None] * expert_out, axis=1).astype(jnp.bfloat16)
    cot_wide = cotangent.astype(jnp.float32)
    d_gates = jnp.sum(cot_wide[:, None, :] * expert_out, axis=2)
    d_out = (gate_vals[:, :, None] * cot_wide[:, None, :]).astype(jnp.bfloat16)
    d_outbox = scatter_rows(d_out, slot_index, total).reshape(groups, capacity, width)
    d_inbox = lax.all_to_all(d_outbox, "expert", split_axis=0, concat_axis=0, tiled=True).reshape(
        total, width
    )
    gate_back, up_back, down_back = (gate_full, up_full, down_full)
    slot_rows = inbox.reshape(total, width)
    hidden_rows = hidden.reshape(total, hid_width)
    d_rows, d_pre_gate, d_pre_up = expert_backward(
        d_inbox,
        pre_gate.reshape(total, hid_width),
        pre_up.reshape(total, hid_width),
        gate_back,
        up_back,
        down_back,
    )
    d_returned = lax.all_to_all(
        d_rows.reshape(groups, capacity, width), "expert", split_axis=0, concat_axis=0, tiled=True
    ).reshape(total, width)
    d_expert = jnp.sum(d_returned[slot_index].astype(jnp.float32), axis=1)
    pieces = [
        row_major(contract_rows(slot_rows, d_pre_gate)),
        row_major(contract_rows(slot_rows, d_pre_up)),
        row_major(contract_rows(d_inbox, hidden_rows)),
    ]
    shares = lax.psum_scatter(
        (jnp.concatenate(pieces, axis=1) * grad_scale).astype(jnp.bfloat16),
        "dp",
        scatter_dimension=0,
        tiled=True,
    ).astype(jnp.float32)
    grad_stack = jnp.stack(
        [shares[:, :hid_width], shares[:, hid_width : 2 * hid_width], shares[:, 2 * hid_width :]],
        axis=0,
    ).astype(jnp.bfloat16)
    d_logits = gate_vjp(d_gates)[0].astype(jnp.bfloat16)
    router_term = contract_rows(tokens, d_logits) * router_scale
    router_grad, grad_stack = reduce_router(router_term, grad_stack, partner, my_index)
    router_back = lax.dot_general(
        d_logits, router_weight, (((1,), (1,)), ((), ())), preferred_element_type=jnp.float32
    )
    token_grad = (d_expert + router_back).astype(jnp.bfloat16)
    return (mixed, token_grad, grad_stack[0:1], grad_stack[1:2], grad_stack[2:3], router_grad)


def solution(mesh):
    in_specs = (
        P(("dp", "expert"), None),
        P(("dp", "expert"), None),
        P(("dp", "expert"), None),
        P(),
        P(),
        P("expert", "dp", None),
        P("expert", "dp", None),
        P("expert", "dp", None),
    )
    out_specs = (
        P(("dp", "expert"), None),
        P(("dp", "expert"), None),
        P("expert", "dp", None),
        P("expert", "dp", None),
        P("expert", "dp", None),
        P(),
    )
    return jax.shard_map(
        on_device, mesh=mesh, in_specs=in_specs, out_specs=out_specs, check_vma=False
    )
```

```python
import jax
import jax.numpy as jnp
from jax import lax
from jax.sharding import PartitionSpec as P
from jax.experimental.layout import Layout, with_layout_constraint


def swapped(array, axis, stride):
    return lax.ppermute(array, axis, [(i, i ^ 1 << stride) for i in range(lax.axis_size(axis))])


def gather_by_exchange(piece, axis):
    count = lax.axis_size(axis)
    copies = jnp.broadcast_to(piece[None], (count,) + piece.shape)
    joined = lax.all_to_all(copies, axis, 0, 0, tiled=True)
    return joined.reshape((count * piece.shape[0],) + piece.shape[1:])


def reduce_router(term, companion, partner, my_index):
    groups = lax.axis_size("expert")
    replicas = lax.axis_size("dp")
    rows = term.shape[0]
    parts = lax.all_to_all(
        term.reshape(groups, rows // groups, term.shape[1]), "expert", 0, 0, tiled=True
    )
    piece = jnp.sum(parts, axis=0)
    for bit_level in range(replicas.bit_length() - 1):
        piece = piece + swapped(piece, "dp", bit_level)
    piece, companion = lax.optimization_barrier((piece, companion))
    arrivals = [swapped(companion, "expert", bit_level) for bit_level in range(groups.bit_length() - 1)]
    whole = gather_by_exchange(piece, "expert")
    whole, arrivals = lax.optimization_barrier((whole, arrivals))
    chosen = companion
    for bit_level, arrived in enumerate(arrivals):
        chosen = jnp.where(partner == jnp.bitwise_xor(my_index, 1 << bit_level), arrived, chosen)
    return whole, chosen


def gate_values(logits, picked):
    scores = jax.nn.sigmoid(logits)
    chosen = jnp.sum(scores[:, None, :] * picked, axis=2)
    return chosen / jnp.sum(chosen, axis=1, keepdims=True)


def slot_numbers(expert_ids, holder, capacity, devices):
    labels = jnp.arange(devices, dtype=jnp.int32)
    member_e = (expert_ids[:, :, None] == labels[None, None, :]).astype(jnp.int32)
    target = jnp.sum(member_e * holder[None, None, :], axis=2)
    flat_target = target.reshape(-1)
    member = (flat_target[:, None] == labels[None, :]).astype(jnp.int32)
    ranking = jnp.sum((jnp.cumsum(member, axis=0) - 1) * member, axis=1)
    return (flat_target * capacity + ranking).reshape(expert_ids.shape)


def scatter_rows(per_pair, slot_index, total):
    flat_rows = per_pair.reshape(-1, per_pair.shape[2])
    empty = jnp.zeros((total, per_pair.shape[2]), per_pair.dtype)
    return empty.at[slot_index.reshape(-1)].set(flat_rows)


def expert_forward(slot_rows, gate_full, up_full, down_full):
    pre_gate = jnp.dot(slot_rows, gate_full, preferred_element_type=jnp.float32)
    pre_up = jnp.dot(slot_rows, up_full, preferred_element_type=jnp.float32)
    hidden = (jax.nn.silu(pre_gate) * pre_up).astype(jnp.bfloat16)
    result = lax.dot_general(
        hidden, down_full, (((1,), (1,)), ((), ())), preferred_element_type=jnp.float32
    )
    return (result.astype(jnp.bfloat16), pre_gate, pre_up, hidden)


def expert_backward(d_out, pre_gate, pre_up, gate_full, up_full, down_full):
    d_hidden = jnp.dot(d_out, down_full, preferred_element_type=jnp.float32)
    sigma = jax.nn.sigmoid(pre_gate)
    d_pre_gate = (d_hidden * pre_up * sigma * (1.0 + pre_gate * (1.0 - sigma))).astype(jnp.bfloat16)
    d_pre_up = (d_hidden * pre_gate * sigma).astype(jnp.bfloat16)
    back_dims = (((1,), (1,)), ((), ()))
    d_rows = lax.dot_general(d_pre_gate, gate_full, back_dims, preferred_element_type=jnp.float32)
    d_rows = d_rows + lax.dot_general(
        d_pre_up, up_full, back_dims, preferred_element_type=jnp.float32
    )
    return (d_rows.astype(jnp.bfloat16), d_pre_gate, d_pre_up)


def row_major(array):
    return with_layout_constraint(array, Layout(major_to_minor=tuple(range(array.ndim))))


def contract_rows(left, right):
    return lax.dot_general(
        left, right, (((0,), (0,)), ((), ())), preferred_element_type=jnp.float32
    )


def on_device(
    tokens, cotangent, expert_ids, placed, router_weight, gate_weight, up_weight, down_weight
):
    count = tokens.shape[0]
    width = tokens.shape[1]
    hid_width = gate_weight.shape[2]
    groups = lax.axis_size("expert")
    replicas = lax.axis_size("dp")
    capacity = 3 * count // groups
    total = groups * capacity
    levels = groups.bit_length() - 1
    my_index = lax.axis_index("expert")
    labels = jnp.arange(groups, dtype=jnp.int32)
    partner = jnp.sum(jnp.where(labels == my_index, placed, 0))
    grad_scale = (2.0 * count * replicas) ** (-0.5)
    router_scale = (1.0 * count * replicas * groups) ** (-0.5)
    logits = jnp.dot(tokens, router_weight, preferred_element_type=jnp.float32)
    picked = (expert_ids[:, :, None] == labels[None, None, :]).astype(jnp.float32)

    def gate_of(values):
        return gate_values(values, picked)

    gate_vals, gate_vjp = jax.vjp(gate_of, logits)
    held = jnp.concatenate([gate_weight, up_weight, down_weight], axis=0)
    gathered = lax.all_gather(held, "dp", axis=1, tiled=True)
    gate_full, up_full, down_full = (gathered[0], gathered[1], gathered[2])
    slot_index = slot_numbers(expert_ids, labels, capacity, groups)
    spread = jnp.broadcast_to(tokens[:, None, :], (count, 2, width))
    outbox = scatter_rows(spread, slot_index, total).reshape(groups, capacity, width)
    received = lax.all_to_all(outbox, "expert", split_axis=0, concat_axis=0, tiled=True)
    item_count = received.shape[1]
    forward_slot_rows = received.reshape(-1, width)
    result, pre_gate, pre_up, hidden = expert_forward(
        forward_slot_rows, gate_full, up_full, down_full
    )
    result, pre_gate, pre_up, hidden, inbox = (
        result.reshape(groups, item_count, width),
        pre_gate.reshape(groups, item_count, hid_width),
        pre_up.reshape(groups, item_count, hid_width),
        hidden.reshape(groups, item_count, hid_width),
        received,
    )
    returned = lax.all_to_all(result, "expert", split_axis=0, concat_axis=0, tiled=True).reshape(
        total, width
    )
    expert_out = returned[slot_index].astype(jnp.float32)
    mixed = jnp.sum(gate_vals[:, :, None] * expert_out, axis=1).astype(jnp.bfloat16)
    cot_wide = cotangent.astype(jnp.float32)
    d_gates = jnp.sum(cot_wide[:, None, :] * expert_out, axis=2)
    d_out = (gate_vals[:, :, None] * cot_wide[:, None, :]).astype(jnp.bfloat16)
    d_outbox = scatter_rows(d_out, slot_index, total).reshape(groups, capacity, width)
    d_inbox = lax.all_to_all(d_outbox, "expert", split_axis=0, concat_axis=0, tiled=True).reshape(
        total, width
    )
    gate_back, up_back, down_back = (gate_full, up_full, down_full)
    slot_rows = inbox.reshape(total, width)
    hidden_rows = hidden.reshape(total, hid_width)
    d_rows, d_pre_gate, d_pre_up = expert_backward(
        d_inbox,
        pre_gate.reshape(total, hid_width),
        pre_up.reshape(total, hid_width),
        gate_back,
        up_back,
        down_back,
    )
    d_returned = lax.all_to_all(
        d_rows.reshape(groups, capacity, width), "expert", split_axis=0, concat_axis=0, tiled=True
    ).reshape(total, width)
    d_expert = jnp.sum(d_returned[slot_index].astype(jnp.float32), axis=1)
    pieces = [
        row_major(contract_rows(slot_rows, d_pre_gate)),
        row_major(contract_rows(slot_rows, d_pre_up)),
        row_major(contract_rows(d_inbox, hidden_rows)),
    ]
    shares = lax.psum_scatter(
        (jnp.concatenate(pieces, axis=1) * grad_scale).astype(jnp.bfloat16),
        "dp",
        scatter_dimension=0,
        tiled=True,
    ).astype(jnp.float32)
    grad_stack = jnp.stack(
        [shares[:, :hid_width], shares[:, hid_width : 2 * hid_width], shares[:, 2 * hid_width :]],
        axis=0,
    ).astype(jnp.bfloat16)
    d_logits = gate_vjp(d_gates)[0].astype(jnp.bfloat16)
    router_term = contract_rows(tokens, d_logits) * router_scale
    router_grad, grad_stack = reduce_router(router_term, grad_stack, partner, my_index)
    router_back = lax.dot_general(
        d_logits, router_weight, (((1,), (1,)), ((), ())), preferred_element_type=jnp.float32
    )
    token_grad = (d_expert + router_back).astype(jnp.bfloat16)
    return (mixed, token_grad, grad_stack[0:1], grad_stack[1:2], grad_stack[2:3], router_grad)


def solution(mesh):
    in_specs = (
        P(("dp", "expert"), None),
        P(("dp", "expert"), None),
        P(("dp", "expert"), None),
        P(),
        P(),
        P("expert", "dp", None),
        P("expert", "dp", None),
        P("expert", "dp", None),
    )
    out_specs = (
        P(("dp", "expert"), None),
        P(("dp", "expert"), None),
        P("expert", "dp", None),
        P("expert", "dp", None),
        P("expert", "dp", None),
        P(),
    )
    return jax.shard_map(
        on_device, mesh=mesh, in_specs=in_specs, out_specs=out_specs, check_vma=False
    )
```

```python
import jax
import jax.numpy as jnp
from jax import lax
from jax.sharding import PartitionSpec as P
from jax.experimental.layout import Layout, with_layout_constraint


def swapped(array, axis, stride):
    return lax.ppermute(array, axis, [(i, i ^ 1 << stride) for i in range(lax.axis_size(axis))])


def gather_by_exchange(piece, axis):
    count = lax.axis_size(axis)
    copies = jnp.broadcast_to(piece[None], (count,) + piece.shape)
    joined = lax.all_to_all(copies, axis, 0, 0, tiled=True)
    return joined.reshape((count * piece.shape[0],) + piece.shape[1:])


def reduce_router(term, companion, partner, my_index):
    groups = lax.axis_size("expert")
    replicas = lax.axis_size("dp")
    rows = term.shape[0]
    parts = lax.all_to_all(
        term.reshape(groups, rows // groups, term.shape[1]), "expert", 0, 0, tiled=True
    )
    piece = jnp.sum(parts, axis=0)
    piece, companion = lax.optimization_barrier((piece, companion))
    arrivals = [swapped(companion, "expert", bit_level) for bit_level in range(groups.bit_length() - 1)]
    for bit_level in range(replicas.bit_length() - 1):
        piece = piece + swapped(piece, "dp", bit_level)
    piece, arrivals = lax.optimization_barrier((piece, arrivals))
    chosen = []
    for index in range(companion.shape[0]):
        own = companion[index : index + 1]
        for bit_level, arrived in enumerate(arrivals):
            mate = partner == jnp.bitwise_xor(my_index, 1 << bit_level)
            own = jnp.where(mate, arrived[index : index + 1], own)
        chosen.append(own)
    return gather_by_exchange(piece, "expert"), chosen


def gate_values(logits, picked):
    scores = jax.nn.sigmoid(logits)
    chosen = jnp.sum(scores[:, None, :] * picked, axis=2)
    return chosen / jnp.sum(chosen, axis=1, keepdims=True)


def slot_numbers(expert_ids, holder, capacity, devices):
    labels = jnp.arange(devices, dtype=jnp.int32)
    member_e = (expert_ids[:, :, None] == labels[None, None, :]).astype(jnp.int32)
    target = jnp.sum(member_e * holder[None, None, :], axis=2)
    flat_target = target.reshape(-1)
    member = (flat_target[:, None] == labels[None, :]).astype(jnp.int32)
    ranking = jnp.sum((jnp.cumsum(member, axis=0) - 1) * member, axis=1)
    return (flat_target * capacity + ranking).reshape(expert_ids.shape)


def scatter_rows(per_pair, slot_index, total):
    flat_rows = per_pair.reshape(-1, per_pair.shape[2])
    empty = jnp.zeros((total, per_pair.shape[2]), per_pair.dtype)
    return empty.at[slot_index.reshape(-1)].set(flat_rows)


def expert_forward(slot_rows, gate_full, up_full, down_full):
    pre_gate = jnp.dot(slot_rows, gate_full, preferred_element_type=jnp.float32)
    pre_up = jnp.dot(slot_rows, up_full, preferred_element_type=jnp.float32)
    hidden = (jax.nn.silu(pre_gate) * pre_up).astype(jnp.bfloat16)
    result = lax.dot_general(
        hidden, down_full, (((1,), (1,)), ((), ())), preferred_element_type=jnp.float32
    )
    return (result.astype(jnp.bfloat16), pre_gate, pre_up, hidden)


def expert_backward(d_out, pre_gate, pre_up, gate_full, up_full, down_full):
    d_hidden = jnp.dot(d_out, down_full, preferred_element_type=jnp.float32)
    sigma = jax.nn.sigmoid(pre_gate)
    d_pre_gate = (d_hidden * pre_up * sigma * (1.0 + pre_gate * (1.0 - sigma))).astype(jnp.bfloat16)
    d_pre_up = (d_hidden * pre_gate * sigma).astype(jnp.bfloat16)
    back_dims = (((1,), (1,)), ((), ()))
    d_rows = lax.dot_general(d_pre_gate, gate_full, back_dims, preferred_element_type=jnp.float32)
    d_rows = d_rows + lax.dot_general(
        d_pre_up, up_full, back_dims, preferred_element_type=jnp.float32
    )
    return (d_rows.astype(jnp.bfloat16), d_pre_gate, d_pre_up)


def row_major(array):
    return with_layout_constraint(array, Layout(major_to_minor=tuple(range(array.ndim))))


def contract_rows(left, right):
    return lax.dot_general(
        left, right, (((0,), (0,)), ((), ())), preferred_element_type=jnp.float32
    )


def on_device(
    tokens, cotangent, expert_ids, placed, router_weight, gate_weight, up_weight, down_weight
):
    count = tokens.shape[0]
    width = tokens.shape[1]
    hid_width = gate_weight.shape[2]
    groups = lax.axis_size("expert")
    replicas = lax.axis_size("dp")
    capacity = 3 * count // groups
    total = groups * capacity
    levels = groups.bit_length() - 1
    my_index = lax.axis_index("expert")
    labels = jnp.arange(groups, dtype=jnp.int32)
    partner = jnp.sum(jnp.where(labels == my_index, placed, 0))
    grad_scale = (2.0 * count * replicas) ** (-0.5)
    router_scale = (1.0 * count * replicas * groups) ** (-0.5)
    logits = jnp.dot(tokens, router_weight, preferred_element_type=jnp.float32)
    picked = (expert_ids[:, :, None] == labels[None, None, :]).astype(jnp.float32)

    def gate_of(values):
        return gate_values(values, picked)

    gate_vals, gate_vjp = jax.vjp(gate_of, logits)
    held = jnp.concatenate([gate_weight, up_weight, down_weight], axis=0)
    gathered = lax.all_gather(held, "dp", axis=1, tiled=True)
    gate_full, up_full, down_full = (gathered[0], gathered[1], gathered[2])
    slot_index = slot_numbers(expert_ids, labels, capacity, groups)
    spread = jnp.broadcast_to(tokens[:, None, :], (count, 2, width))
    outbox = scatter_rows(spread, slot_index, total).reshape(groups, capacity, width)
    received = lax.all_to_all(outbox, "expert", split_axis=0, concat_axis=0, tiled=True)
    item_count = received.shape[1]
    forward_slot_rows = received.reshape(-1, width)
    result, pre_gate, pre_up, hidden = expert_forward(
        forward_slot_rows, gate_full, up_full, down_full
    )
    result, pre_gate, pre_up, hidden, inbox = (
        result.reshape(groups, item_count, width),
        pre_gate.reshape(groups, item_count, hid_width),
        pre_up.reshape(groups, item_count, hid_width),
        hidden.reshape(groups, item_count, hid_width),
        received,
    )
    returned = lax.all_to_all(result, "expert", split_axis=0, concat_axis=0, tiled=True).reshape(
        total, width
    )
    expert_out = returned[slot_index].astype(jnp.float32)
    mixed = jnp.sum(gate_vals[:, :, None] * expert_out, axis=1).astype(jnp.bfloat16)
    cot_wide = cotangent.astype(jnp.float32)
    d_gates = jnp.sum(cot_wide[:, None, :] * expert_out, axis=2)
    d_out = (gate_vals[:, :, None] * cot_wide[:, None, :]).astype(jnp.bfloat16)
    d_outbox = scatter_rows(d_out, slot_index, total).reshape(groups, capacity, width)
    d_inbox = lax.all_to_all(d_outbox, "expert", split_axis=0, concat_axis=0, tiled=True).reshape(
        total, width
    )
    gate_back, up_back, down_back = (gate_full, up_full, down_full)
    slot_rows = inbox.reshape(total, width)
    hidden_rows = hidden.reshape(total, hid_width)
    d_rows, d_pre_gate, d_pre_up = expert_backward(
        d_inbox,
        pre_gate.reshape(total, hid_width),
        pre_up.reshape(total, hid_width),
        gate_back,
        up_back,
        down_back,
    )
    d_returned = lax.all_to_all(
        d_rows.reshape(groups, capacity, width), "expert", split_axis=0, concat_axis=0, tiled=True
    ).reshape(total, width)
    d_expert = jnp.sum(d_returned[slot_index].astype(jnp.float32), axis=1)
    pieces = [
        row_major(contract_rows(slot_rows, d_pre_gate)),
        row_major(contract_rows(slot_rows, d_pre_up)),
        row_major(contract_rows(d_inbox, hidden_rows)),
    ]
    shares = lax.psum_scatter(
        (jnp.concatenate(pieces, axis=1) * grad_scale).astype(jnp.bfloat16),
        "dp",
        scatter_dimension=0,
        tiled=True,
    ).astype(jnp.float32)
    grad_stack = jnp.stack(
        [shares[:, :hid_width], shares[:, hid_width : 2 * hid_width], shares[:, 2 * hid_width :]],
        axis=0,
    ).astype(jnp.bfloat16)
    d_logits = gate_vjp(d_gates)[0].astype(jnp.bfloat16)
    router_term = contract_rows(tokens, d_logits) * router_scale
    router_grad, grad_stack = reduce_router(router_term, grad_stack, partner, my_index)
    router_back = lax.dot_general(
        d_logits, router_weight, (((1,), (1,)), ((), ())), preferred_element_type=jnp.float32
    )
    token_grad = (d_expert + router_back).astype(jnp.bfloat16)
    return (mixed, token_grad, grad_stack[0], grad_stack[1], grad_stack[2], router_grad)


def solution(mesh):
    in_specs = (
        P(("dp", "expert"), None),
        P(("dp", "expert"), None),
        P(("dp", "expert"), None),
        P(),
        P(),
        P("expert", "dp", None),
        P("expert", "dp", None),
        P("expert", "dp", None),
    )
    out_specs = (
        P(("dp", "expert"), None),
        P(("dp", "expert"), None),
        P("expert", "dp", None),
        P("expert", "dp", None),
        P("expert", "dp", None),
        P(),
    )
    return jax.shard_map(
        on_device, mesh=mesh, in_specs=in_specs, out_specs=out_specs, check_vma=False
    )
```

```python
import jax
import jax.numpy as jnp
from jax import lax
from jax.sharding import PartitionSpec as P
from jax.experimental.layout import Layout, with_layout_constraint


def swapped(array, axis, stride):
    return lax.ppermute(array, axis, [(i, i ^ 1 << stride) for i in range(lax.axis_size(axis))])


def gather_by_exchange(piece, axis):
    count = lax.axis_size(axis)
    copies = jnp.broadcast_to(piece[None], (count,) + piece.shape)
    joined = lax.all_to_all(copies, axis, 0, 0, tiled=True)
    return joined.reshape((count * piece.shape[0],) + piece.shape[1:])


def reduce_router(term, companion, partner, my_index):
    groups = lax.axis_size("expert")
    replicas = lax.axis_size("dp")
    rows = term.shape[0]
    parts = lax.all_to_all(
        term.reshape(groups, rows // groups, term.shape[1]), "expert", 0, 0, tiled=True
    )
    piece = jnp.sum(parts, axis=0)
    piece, companion = lax.optimization_barrier((piece, companion))
    arrivals = [swapped(companion, "expert", bit_level) for bit_level in range(groups.bit_length() - 1)]
    for bit_level in range(replicas.bit_length() - 1):
        piece = piece + swapped(piece, "dp", bit_level)
    piece, arrivals = lax.optimization_barrier((piece, arrivals))
    chosen = companion
    for bit_level, arrived in enumerate(arrivals):
        chosen = jnp.where(partner == jnp.bitwise_xor(my_index, 1 << bit_level), arrived, chosen)
    return gather_by_exchange(piece, "expert"), chosen


def gate_values(logits, picked):
    scores = jax.nn.sigmoid(logits)
    chosen = jnp.sum(scores[:, None, :] * picked, axis=2)
    return chosen / jnp.sum(chosen, axis=1, keepdims=True)


def slot_numbers(expert_ids, holder, capacity, devices):
    labels = jnp.arange(devices, dtype=jnp.int32)
    member_e = (expert_ids[:, :, None] == labels[None, None, :]).astype(jnp.int32)
    target = jnp.sum(member_e * holder[None, None, :], axis=2)
    flat_target = target.reshape(-1)
    member = (flat_target[:, None] == labels[None, :]).astype(jnp.int32)
    ranking = jnp.sum((jnp.cumsum(member, axis=0) - 1) * member, axis=1)
    return (flat_target * capacity + ranking).reshape(expert_ids.shape)


def scatter_rows(per_pair, slot_index, total):
    flat_rows = per_pair.reshape(-1, per_pair.shape[2])
    empty = jnp.zeros((total, per_pair.shape[2]), per_pair.dtype)
    return empty.at[slot_index.reshape(-1)].set(flat_rows)


def expert_forward(slot_rows, gate_full, up_full, down_full):
    pre_gate = jnp.dot(slot_rows, gate_full, preferred_element_type=jnp.float32)
    pre_up = jnp.dot(slot_rows, up_full, preferred_element_type=jnp.float32)
    hidden = (jax.nn.silu(pre_gate) * pre_up).astype(jnp.bfloat16)
    result = lax.dot_general(
        hidden, down_full, (((1,), (1,)), ((), ())), preferred_element_type=jnp.float32
    )
    return (result.astype(jnp.bfloat16), pre_gate, pre_up, hidden)


def expert_backward(d_out, pre_gate, pre_up, gate_full, up_full, down_full):
    d_hidden = jnp.dot(d_out, down_full, preferred_element_type=jnp.float32)
    sigma = jax.nn.sigmoid(pre_gate)
    d_pre_gate = (d_hidden * pre_up * sigma * (1.0 + pre_gate * (1.0 - sigma))).astype(jnp.bfloat16)
    d_pre_up = (d_hidden * pre_gate * sigma).astype(jnp.bfloat16)
    back_dims = (((1,), (1,)), ((), ()))
    d_rows = lax.dot_general(d_pre_gate, gate_full, back_dims, preferred_element_type=jnp.float32)
    d_rows = d_rows + lax.dot_general(
        d_pre_up, up_full, back_dims, preferred_element_type=jnp.float32
    )
    return (d_rows.astype(jnp.bfloat16), d_pre_gate, d_pre_up)


def row_major(array):
    return with_layout_constraint(array, Layout(major_to_minor=tuple(range(array.ndim))))


def contract_rows(left, right):
    return lax.dot_general(
        left, right, (((0,), (0,)), ((), ())), preferred_element_type=jnp.float32
    )


def on_device(
    tokens, cotangent, expert_ids, placed, router_weight, gate_weight, up_weight, down_weight
):
    count = tokens.shape[0]
    width = tokens.shape[1]
    hid_width = gate_weight.shape[2]
    groups = lax.axis_size("expert")
    replicas = lax.axis_size("dp")
    capacity = 3 * count // groups
    total = groups * capacity
    levels = groups.bit_length() - 1
    my_index = lax.axis_index("expert")
    labels = jnp.arange(groups, dtype=jnp.int32)
    partner = jnp.sum(jnp.where(labels == my_index, placed, 0))
    grad_scale = (2.0 * count * replicas) ** (-0.5)
    router_scale = (1.0 * count * replicas * groups) ** (-0.5)
    logits = jnp.dot(tokens, router_weight, preferred_element_type=jnp.float32)
    picked = (expert_ids[:, :, None] == labels[None, None, :]).astype(jnp.float32)

    def gate_of(values):
        return gate_values(values, picked)

    gate_vals, gate_vjp = jax.vjp(gate_of, logits)
    held = jnp.concatenate([gate_weight, up_weight, down_weight], axis=0)
    gathered = lax.all_gather(held, "dp", axis=1, tiled=True)
    gate_full, up_full, down_full = (gathered[0], gathered[1], gathered[2])
    slot_index = slot_numbers(expert_ids, labels, capacity, groups)
    spread = jnp.broadcast_to(tokens[:, None, :], (count, 2, width))
    outbox = scatter_rows(spread, slot_index, total).reshape(groups, capacity, width)
    received = lax.all_to_all(outbox, "expert", split_axis=0, concat_axis=0, tiled=True)
    item_count = received.shape[1]
    forward_slot_rows = received.reshape(-1, width)
    result, pre_gate, pre_up, hidden = expert_forward(
        forward_slot_rows, gate_full, up_full, down_full
    )
    result, pre_gate, pre_up, hidden, inbox = (
        result.reshape(groups, item_count, width),
        pre_gate.reshape(groups, item_count, hid_width),
        pre_up.reshape(groups, item_count, hid_width),
        hidden.reshape(groups, item_count, hid_width),
        received,
    )
    returned = lax.all_to_all(result, "expert", split_axis=0, concat_axis=0, tiled=True).reshape(
        total, width
    )
    expert_out = returned[slot_index].astype(jnp.float32)
    mixed = jnp.sum(gate_vals[:, :, None] * expert_out, axis=1).astype(jnp.bfloat16)
    cot_wide = cotangent.astype(jnp.float32)
    d_gates = jnp.sum(cot_wide[:, None, :] * expert_out, axis=2)
    d_out = (gate_vals[:, :, None] * cot_wide[:, None, :]).astype(jnp.bfloat16)
    d_outbox = scatter_rows(d_out, slot_index, total).reshape(groups, capacity, width)
    d_inbox = lax.all_to_all(d_outbox, "expert", split_axis=0, concat_axis=0, tiled=True).reshape(
        total, width
    )
    gate_back, up_back, down_back = (gate_full, up_full, down_full)
    slot_rows = inbox.reshape(total, width)
    hidden_rows = hidden.reshape(total, hid_width)
    d_rows, d_pre_gate, d_pre_up = expert_backward(
        d_inbox,
        pre_gate.reshape(total, hid_width),
        pre_up.reshape(total, hid_width),
        gate_back,
        up_back,
        down_back,
    )
    d_returned = lax.all_to_all(
        d_rows.reshape(groups, capacity, width), "expert", split_axis=0, concat_axis=0, tiled=True
    ).reshape(total, width)
    d_expert = jnp.sum(d_returned[slot_index].astype(jnp.float32), axis=1)
    pieces = [
        row_major(contract_rows(slot_rows, jnp.concatenate([d_pre_gate, d_pre_up], axis=1))),
        row_major(contract_rows(d_inbox, hidden_rows)),
    ]
    shares = lax.psum_scatter(
        (jnp.concatenate(pieces, axis=1) * grad_scale).astype(jnp.bfloat16),
        "dp",
        scatter_dimension=0,
        tiled=True,
    ).astype(jnp.float32)
    grad_stack = jnp.stack(
        [shares[:, :hid_width], shares[:, hid_width : 2 * hid_width], shares[:, 2 * hid_width :]],
        axis=0,
    ).astype(jnp.bfloat16)
    d_logits = gate_vjp(d_gates)[0].astype(jnp.bfloat16)
    router_term = contract_rows(tokens, d_logits) * router_scale
    router_grad, grad_stack = reduce_router(router_term, grad_stack, partner, my_index)
    router_back = lax.dot_general(
        d_logits, router_weight, (((1,), (1,)), ((), ())), preferred_element_type=jnp.float32
    )
    token_grad = (d_expert + router_back).astype(jnp.bfloat16)
    return (mixed, token_grad, grad_stack[0:1], grad_stack[1:2], grad_stack[2:3], router_grad)


def solution(mesh):
    in_specs = (
        P(("dp", "expert"), None),
        P(("dp", "expert"), None),
        P(("dp", "expert"), None),
        P(),
        P(),
        P("expert", "dp", None),
        P("expert", "dp", None),
        P("expert", "dp", None),
    )
    out_specs = (
        P(("dp", "expert"), None),
        P(("dp", "expert"), None),
        P("expert", "dp", None),
        P("expert", "dp", None),
        P("expert", "dp", None),
        P(),
    )
    return jax.shard_map(
        on_device, mesh=mesh, in_specs=in_specs, out_specs=out_specs, check_vma=False
    )
```

```python
import jax
import jax.numpy as jnp
from jax import lax
from jax.sharding import PartitionSpec as P
from jax.experimental.layout import Layout, with_layout_constraint


def swapped(array, axis, stride):
    return lax.ppermute(array, axis, [(i, i ^ 1 << stride) for i in range(lax.axis_size(axis))])


def gather_by_exchange(piece, axis):
    count = lax.axis_size(axis)
    copies = jnp.broadcast_to(piece[None], (count,) + piece.shape)
    joined = lax.all_to_all(copies, axis, 0, 0, tiled=True)
    return joined.reshape((count * piece.shape[0],) + piece.shape[1:])


def reduce_router(term, companion, partner, my_index):
    groups = lax.axis_size("expert")
    replicas = lax.axis_size("dp")
    rows = term.shape[0]
    parts = lax.all_to_all(
        term.reshape(groups, rows // groups, term.shape[1]), "expert", 0, 0, tiled=True
    )
    piece = jnp.sum(parts, axis=0)
    piece, companion = lax.optimization_barrier((piece, companion))
    arrivals = [swapped(companion, "expert", bit_level) for bit_level in range(groups.bit_length() - 1)][::-1]
    for bit_level in range(replicas.bit_length() - 1):
        piece = piece + swapped(piece, "dp", bit_level)
    piece, arrivals = lax.optimization_barrier((piece, arrivals))
    chosen = companion
    for bit_level, arrived in zip(range(len(arrivals) - 1, -1, -1), arrivals):
        chosen = jnp.where(partner == jnp.bitwise_xor(my_index, 1 << bit_level), arrived, chosen)
    return gather_by_exchange(piece, "expert"), chosen


def gate_values(logits, picked):
    scores = jax.nn.sigmoid(logits)
    chosen = jnp.sum(scores[:, None, :] * picked, axis=2)
    return chosen / jnp.sum(chosen, axis=1, keepdims=True)


def slot_numbers(expert_ids, holder, capacity, devices):
    labels = jnp.arange(devices, dtype=jnp.int32)
    member_e = (expert_ids[:, :, None] == labels[None, None, :]).astype(jnp.int32)
    target = jnp.sum(member_e * holder[None, None, :], axis=2)
    flat_target = target.reshape(-1)
    member = (flat_target[:, None] == labels[None, :]).astype(jnp.int32)
    ranking = jnp.sum((jnp.cumsum(member, axis=0) - 1) * member, axis=1)
    return (flat_target * capacity + ranking).reshape(expert_ids.shape)


def scatter_rows(per_pair, slot_index, total):
    flat_rows = per_pair.reshape(-1, per_pair.shape[2])
    empty = jnp.zeros((total, per_pair.shape[2]), per_pair.dtype)
    return empty.at[slot_index.reshape(-1)].set(flat_rows)


def expert_forward(slot_rows, gate_full, up_full, down_full):
    pre_gate = jnp.dot(slot_rows, gate_full, preferred_element_type=jnp.float32)
    pre_up = jnp.dot(slot_rows, up_full, preferred_element_type=jnp.float32)
    hidden = (jax.nn.silu(pre_gate) * pre_up).astype(jnp.bfloat16)
    result = lax.dot_general(
        hidden, down_full, (((1,), (1,)), ((), ())), preferred_element_type=jnp.float32
    )
    return (result.astype(jnp.bfloat16), pre_gate, pre_up, hidden)


def expert_backward(d_out, pre_gate, pre_up, gate_full, up_full, down_full):
    d_hidden = jnp.dot(d_out, down_full, preferred_element_type=jnp.float32)
    sigma = jax.nn.sigmoid(pre_gate)
    d_pre_gate = (d_hidden * pre_up * sigma * (1.0 + pre_gate * (1.0 - sigma))).astype(jnp.bfloat16)
    d_pre_up = (d_hidden * pre_gate * sigma).astype(jnp.bfloat16)
    back_dims = (((1,), (1,)), ((), ()))
    d_rows = lax.dot_general(d_pre_gate, gate_full, back_dims, preferred_element_type=jnp.float32)
    d_rows = d_rows + lax.dot_general(
        d_pre_up, up_full, back_dims, preferred_element_type=jnp.float32
    )
    return (d_rows.astype(jnp.bfloat16), d_pre_gate, d_pre_up)


def row_major(array):
    return with_layout_constraint(array, Layout(major_to_minor=tuple(range(array.ndim))))


def contract_rows(left, right):
    return lax.dot_general(
        left, right, (((0,), (0,)), ((), ())), preferred_element_type=jnp.float32
    )


def on_device(
    tokens, cotangent, expert_ids, placed, router_weight, gate_weight, up_weight, down_weight
):
    count = tokens.shape[0]
    width = tokens.shape[1]
    hid_width = gate_weight.shape[2]
    groups = lax.axis_size("expert")
    replicas = lax.axis_size("dp")
    capacity = 3 * count // groups
    total = groups * capacity
    levels = groups.bit_length() - 1
    my_index = lax.axis_index("expert")
    labels = jnp.arange(groups, dtype=jnp.int32)
    partner = jnp.sum(jnp.where(labels == my_index, placed, 0))
    grad_scale = (2.0 * count * replicas) ** (-0.5)
    router_scale = (1.0 * count * replicas * groups) ** (-0.5)
    logits = jnp.dot(tokens, router_weight, preferred_element_type=jnp.float32)
    picked = (expert_ids[:, :, None] == labels[None, None, :]).astype(jnp.float32)

    def gate_of(values):
        return gate_values(values, picked)

    gate_vals, gate_vjp = jax.vjp(gate_of, logits)
    held = jnp.concatenate([gate_weight, up_weight, down_weight], axis=0)
    gathered = lax.all_gather(held, "dp", axis=1, tiled=True)
    gate_full, up_full, down_full = (gathered[0], gathered[1], gathered[2])
    slot_index = slot_numbers(expert_ids, labels, capacity, groups)
    spread = jnp.broadcast_to(tokens[:, None, :], (count, 2, width))
    outbox = scatter_rows(spread, slot_index, total).reshape(groups, capacity, width)
    received = lax.all_to_all(outbox, "expert", split_axis=0, concat_axis=0, tiled=True)
    item_count = received.shape[1]
    forward_slot_rows = received.reshape(-1, width)
    result, pre_gate, pre_up, hidden = expert_forward(
        forward_slot_rows, gate_full, up_full, down_full
    )
    result, pre_gate, pre_up, hidden, inbox = (
        result.reshape(groups, item_count, width),
        pre_gate.reshape(groups, item_count, hid_width),
        pre_up.reshape(groups, item_count, hid_width),
        hidden.reshape(groups, item_count, hid_width),
        received,
    )
    returned = lax.all_to_all(result, "expert", split_axis=0, concat_axis=0, tiled=True).reshape(
        total, width
    )
    expert_out = returned[slot_index].astype(jnp.float32)
    mixed = jnp.sum(gate_vals[:, :, None] * expert_out, axis=1).astype(jnp.bfloat16)
    cot_wide = cotangent.astype(jnp.float32)
    d_gates = jnp.sum(cot_wide[:, None, :] * expert_out, axis=2)
    d_out = (gate_vals[:, :, None] * cot_wide[:, None, :]).astype(jnp.bfloat16)
    d_outbox = scatter_rows(d_out, slot_index, total).reshape(groups, capacity, width)
    d_inbox = lax.all_to_all(d_outbox, "expert", split_axis=0, concat_axis=0, tiled=True).reshape(
        total, width
    )
    gate_back, up_back, down_back = (gate_full, up_full, down_full)
    slot_rows = inbox.reshape(total, width)
    hidden_rows = hidden.reshape(total, hid_width)
    d_rows, d_pre_gate, d_pre_up = expert_backward(
        d_inbox,
        pre_gate.reshape(total, hid_width),
        pre_up.reshape(total, hid_width),
        gate_back,
        up_back,
        down_back,
    )
    d_returned = lax.all_to_all(
        d_rows.reshape(groups, capacity, width), "expert", split_axis=0, concat_axis=0, tiled=True
    ).reshape(total, width)
    d_expert = jnp.sum(d_returned[slot_index].astype(jnp.float32), axis=1)
    pieces = [
        row_major(contract_rows(slot_rows, jnp.concatenate([d_pre_gate, d_pre_up], axis=1))),
        row_major(contract_rows(d_inbox, hidden_rows)),
    ]
    shares = lax.psum_scatter(
        (jnp.concatenate(pieces, axis=1) * grad_scale).astype(jnp.bfloat16),
        "dp",
        scatter_dimension=0,
        tiled=True,
    ).astype(jnp.float32)
    grad_stack = jnp.stack(
        [shares[:, :hid_width], shares[:, hid_width : 2 * hid_width], shares[:, 2 * hid_width :]],
        axis=0,
    ).astype(jnp.bfloat16)
    d_logits = gate_vjp(d_gates)[0].astype(jnp.bfloat16)
    router_term = contract_rows(tokens, d_logits) * router_scale
    router_grad, grad_stack = reduce_router(router_term, grad_stack, partner, my_index)
    router_back = lax.dot_general(
        d_logits, router_weight, (((1,), (1,)), ((), ())), preferred_element_type=jnp.float32
    )
    token_grad = (d_expert + router_back).astype(jnp.bfloat16)
    return (mixed, token_grad, grad_stack[0:1], grad_stack[1:2], grad_stack[2:3], router_grad)


def solution(mesh):
    in_specs = (
        P(("dp", "expert"), None),
        P(("dp", "expert"), None),
        P(("dp", "expert"), None),
        P(),
        P(),
        P("expert", "dp", None),
        P("expert", "dp", None),
        P("expert", "dp", None),
    )
    out_specs = (
        P(("dp", "expert"), None),
        P(("dp", "expert"), None),
        P("expert", "dp", None),
        P("expert", "dp", None),
        P("expert", "dp", None),
        P(),
    )
    return jax.shard_map(
        on_device, mesh=mesh, in_specs=in_specs, out_specs=out_specs, check_vma=False
    )
```

```python
import jax
import jax.numpy as jnp
from jax import lax
from jax.sharding import PartitionSpec as P
from jax.experimental.layout import Layout, with_layout_constraint


def swapped(array, axis, stride):
    return lax.ppermute(array, axis, [(i, i ^ 1 << stride) for i in range(lax.axis_size(axis))])


def gather_by_exchange(piece, axis):
    count = lax.axis_size(axis)
    copies = jnp.broadcast_to(piece[None], (count,) + piece.shape)
    joined = lax.all_to_all(copies, axis, 0, 0, tiled=True)
    return joined.reshape((count * piece.shape[0],) + piece.shape[1:])


def reduce_router(term, companion, partner, my_index):
    groups = lax.axis_size("expert")
    replicas = lax.axis_size("dp")
    rows = term.shape[0]
    parts = lax.all_to_all(
        term.reshape(groups, rows // groups, term.shape[1]), "expert", 0, 0, tiled=True
    )
    piece = jnp.sum(parts, axis=0)
    piece, companion = lax.optimization_barrier((piece, companion))
    arrivals = [swapped(companion, "expert", bit_level) for bit_level in range(groups.bit_length() - 1)]
    for bit_level in range(replicas.bit_length() - 1):
        piece = piece + swapped(piece, "dp", bit_level)
    piece, arrivals = lax.optimization_barrier((piece, arrivals))
    chosen = companion
    for bit_level, arrived in enumerate(arrivals):
        chosen = jnp.where(partner == jnp.bitwise_xor(my_index, 1 << bit_level), arrived, chosen)
    return gather_by_exchange(piece, "expert"), chosen


def gate_values(logits, picked):
    scores = jax.nn.sigmoid(logits)
    chosen = jnp.sum(scores[:, None, :] * picked, axis=2)
    return chosen / jnp.sum(chosen, axis=1, keepdims=True)


def slot_numbers(expert_ids, holder, capacity, devices):
    labels = jnp.arange(devices, dtype=jnp.int32)
    member_e = (expert_ids[:, :, None] == labels[None, None, :]).astype(jnp.int32)
    target = jnp.sum(member_e * holder[None, None, :], axis=2)
    flat_target = target.reshape(-1)
    member = (flat_target[:, None] == labels[None, :]).astype(jnp.int32)
    ranking = jnp.sum((jnp.cumsum(member, axis=0) - 1) * member, axis=1)
    return (flat_target * capacity + ranking).reshape(expert_ids.shape)


def scatter_rows(per_pair, slot_index, total):
    flat_rows = per_pair.reshape(-1, per_pair.shape[2])
    empty = jnp.zeros((total, per_pair.shape[2]), per_pair.dtype)
    return empty.at[slot_index.reshape(-1)].set(flat_rows)


def expert_forward(slot_rows, gate_full, up_full, down_full):
    pre_gate = jnp.dot(slot_rows, gate_full, preferred_element_type=jnp.float32)
    pre_up = jnp.dot(slot_rows, up_full, preferred_element_type=jnp.float32)
    hidden = (jax.nn.silu(pre_gate) * pre_up).astype(jnp.bfloat16)
    result = lax.dot_general(
        hidden, down_full, (((1,), (1,)), ((), ())), preferred_element_type=jnp.float32
    )
    return (result.astype(jnp.bfloat16), pre_gate, pre_up, hidden)


def expert_backward(d_out, pre_gate, pre_up, gate_full, up_full, down_full):
    d_hidden = jnp.dot(d_out, down_full, preferred_element_type=jnp.float32)
    sigma = jax.nn.sigmoid(pre_gate)
    d_pre_gate = (d_hidden * pre_up * sigma * (1.0 + pre_gate * (1.0 - sigma))).astype(jnp.bfloat16)
    d_pre_up = (d_hidden * pre_gate * sigma).astype(jnp.bfloat16)
    back_dims = (((1,), (1,)), ((), ()))
    d_rows = lax.dot_general(d_pre_gate, gate_full, back_dims, preferred_element_type=jnp.float32)
    d_rows = d_rows + lax.dot_general(
        d_pre_up, up_full, back_dims, preferred_element_type=jnp.float32
    )
    return (d_rows.astype(jnp.bfloat16), d_pre_gate, d_pre_up)


def row_major(array):
    return with_layout_constraint(array, Layout(major_to_minor=tuple(range(array.ndim))))


def contract_rows(left, right):
    return lax.dot_general(
        left, right, (((0,), (0,)), ((), ())), preferred_element_type=jnp.float32
    )


def on_device(
    tokens, cotangent, expert_ids, placed, router_weight, gate_weight, up_weight, down_weight
):
    count = tokens.shape[0]
    width = tokens.shape[1]
    hid_width = gate_weight.shape[2]
    groups = lax.axis_size("expert")
    replicas = lax.axis_size("dp")
    capacity = 3 * count // groups
    total = groups * capacity
    levels = groups.bit_length() - 1
    my_index = lax.axis_index("expert")
    labels = jnp.arange(groups, dtype=jnp.int32)
    partner = jnp.sum(jnp.where(labels == my_index, placed, 0))
    grad_scale = (2.0 * count * replicas) ** (-0.5)
    router_scale = (1.0 * count * replicas * groups) ** (-0.5)
    logits = jnp.dot(tokens, router_weight, preferred_element_type=jnp.float32)
    picked = (expert_ids[:, :, None] == labels[None, None, :]).astype(jnp.float32)

    def gate_of(values):
        return gate_values(values, picked)

    gate_vals, gate_vjp = jax.vjp(gate_of, logits)
    held = jnp.concatenate([gate_weight, up_weight, down_weight], axis=0)
    gathered = lax.all_gather(held, "dp", axis=1, tiled=True)
    gate_full, up_full, down_full = (gathered[0], gathered[1], gathered[2])
    slot_index = slot_numbers(expert_ids, labels, capacity, groups)
    spread = jnp.broadcast_to(tokens[:, None, :], (count, 2, width))
    outbox = scatter_rows(spread, slot_index, total).reshape(groups, capacity, width)
    received = lax.all_to_all(outbox, "expert", split_axis=0, concat_axis=0, tiled=True)
    item_count = received.shape[1]
    forward_slot_rows = received.reshape(-1, width)
    result, pre_gate, pre_up, hidden = expert_forward(
        forward_slot_rows, gate_full, up_full, down_full
    )
    result, pre_gate, pre_up, hidden, inbox = (
        result.reshape(groups, item_count, width),
        pre_gate.reshape(groups, item_count, hid_width),
        pre_up.reshape(groups, item_count, hid_width),
        hidden.reshape(groups, item_count, hid_width),
        received,
    )
    returned = lax.all_to_all(result, "expert", split_axis=0, concat_axis=0, tiled=True).reshape(
        total, width
    )
    expert_out = returned[slot_index].astype(jnp.float32)
    mixed = jnp.sum(gate_vals[:, :, None] * expert_out, axis=1).astype(jnp.bfloat16)
    cot_wide = cotangent.astype(jnp.float32)
    d_gates = jnp.sum(cot_wide[:, None, :] * expert_out, axis=2)
    d_out = (gate_vals[:, :, None] * cot_wide[:, None, :]).astype(jnp.bfloat16)
    d_outbox = scatter_rows(d_out, slot_index, total).reshape(groups, capacity, width)
    d_inbox = lax.all_to_all(d_outbox, "expert", split_axis=0, concat_axis=0, tiled=True).reshape(
        total, width
    )
    gate_back, up_back, down_back = (gate_full, up_full, down_full)
    slot_rows = inbox.reshape(total, width)
    hidden_rows = hidden.reshape(total, hid_width)
    d_rows, d_pre_gate, d_pre_up = expert_backward(
        d_inbox,
        pre_gate.reshape(total, hid_width),
        pre_up.reshape(total, hid_width),
        gate_back,
        up_back,
        down_back,
    )
    d_returned = lax.all_to_all(
        d_rows.reshape(groups, capacity, width), "expert", split_axis=0, concat_axis=0, tiled=True
    ).reshape(total, width)
    d_expert = jnp.sum(d_returned[slot_index].astype(jnp.float32), axis=1)
    joined = jnp.concatenate([d_pre_gate, d_pre_up], axis=1)
    pieces = [
        row_major((contract_rows(slot_rows, joined) * grad_scale).astype(jnp.bfloat16)),
        row_major((contract_rows(d_inbox, hidden_rows) * grad_scale).astype(jnp.bfloat16)),
    ]
    shares = lax.psum_scatter(
        jnp.concatenate(pieces, axis=1),
        "dp",
        scatter_dimension=0,
        tiled=True,
    ).astype(jnp.float32)
    grad_stack = jnp.stack(
        [shares[:, :hid_width], shares[:, hid_width : 2 * hid_width], shares[:, 2 * hid_width :]],
        axis=0,
    ).astype(jnp.bfloat16)
    d_logits = gate_vjp(d_gates)[0].astype(jnp.bfloat16)
    router_term = contract_rows(tokens, d_logits) * router_scale
    router_grad, grad_stack = reduce_router(router_term, grad_stack, partner, my_index)
    router_back = lax.dot_general(
        d_logits, router_weight, (((1,), (1,)), ((), ())), preferred_element_type=jnp.float32
    )
    token_grad = (d_expert + router_back).astype(jnp.bfloat16)
    return (mixed, token_grad, grad_stack[0:1], grad_stack[1:2], grad_stack[2:3], router_grad)


def solution(mesh):
    in_specs = (
        P(("dp", "expert"), None),
        P(("dp", "expert"), None),
        P(("dp", "expert"), None),
        P(),
        P(),
        P("expert", "dp", None),
        P("expert", "dp", None),
        P("expert", "dp", None),
    )
    out_specs = (
        P(("dp", "expert"), None),
        P(("dp", "expert"), None),
        P("expert", "dp", None),
        P("expert", "dp", None),
        P("expert", "dp", None),
        P(),
    )
    return jax.shard_map(
        on_device, mesh=mesh, in_specs=in_specs, out_specs=out_specs, check_vma=False
    )
```
